256 devices in a mesh: row: 8 (over z_hi, x), col: 32 (over z_lo, y, core).
Axes of the slice: x: 4, y: 4, z: 8 (z_hi: 2, z_lo: 4; z = z_hi * 4 + z_lo), core: 2. Of those that a mesh axis runs over, the one named last changes fastest.
Arguments:
- region_factors: bfloat16 [262144, 512], P(('row', 'col')), may hold values from -1.25 to 1.25
- item_factors: bfloat16 [32, 128, 512], P('col', 'row'), may hold values from -1.25 to 1.25
- slab_blocks: bfloat16 [256, 32, 6, 128, 128], P(('row', 'col')), may hold values from -6 to 6
- block_rows: int32 [256, 32, 6], P(('row', 'col')), may hold values from 0 to 7, as said below
- counts: int32 [256, 32], P(('row', 'col')), may hold values from 1 to 6, as said below
Outputs:
- new_regions: float32 [262144, 512], P(('row', 'col'))
- new_items: float32 [32, 128, 512], P('col', 'row')
The draws below stay inside these ranges and needn't reach their ends.
Inputs may be any that keep to these rules, and one draw needn't show every extreme that they name: `counts`: every entry is at least 1; some device-block has exactly 6 present blocks in some block column. `block_rows`: for each device-block and block column, the first counts[d, p] entries are distinct; entries at slots s >= counts[d, p] (and their slab blocks) are not used.
All inputs are finite; a program needn't handle non-finite values.
Results may differ from the reference program's by a relative error of at most 0.0023.
Values may be sent and summed in bfloat16 or wider, within the bound.
No kernel may reach another device: no remote copies, remote signals or barrier semaphores. Data moves between devices by JAX's collectives and lax.ppermute only.
A program may use at most 128 MiB of HBM per device.

```python
import jax
import jax.numpy as jnp
from jax import lax

RANK = 512
BLOCK = 128
RB_DEV = 8
PCAP = 6
PANELS = 32
REGIONS = 262144
DEVICES = 256


def draw_block_rows(key, part):
    key_rows = jax.random.fold_in(key, 17)
    scores = jax.random.randint(key_rows, (DEVICES, PANELS, RB_DEV), 0, 1 << 20) * RB_DEV
    scores = scores + jnp.arange(RB_DEV, dtype=jnp.int32)
    ranking = jnp.argsort(scores, axis=-1)
    return ranking[:, :, :PCAP].astype(jnp.int32)


def draw_counts(key, part):
    key_counts = jax.random.fold_in(key, 29)
    key_level, key_drawn, key_device, key_column = jax.random.split(key_counts, 4)
    density = jax.random.randint(key_level, (DEVICES, 1), 1, PCAP + 1)
    drawn = jax.random.randint(key_drawn, (DEVICES, PANELS), 1, density + 1)
    busy_device = jax.random.randint(key_device, (), 0, DEVICES)
    busy_column = jax.random.randint(key_column, (), 0, PANELS)
    chosen_cell = (jnp.arange(DEVICES, dtype=jnp.int32)[:, None] == busy_device) & (jnp.arange(PANELS, dtype=jnp.int32)[None, :] == busy_column)
    return jnp.where(chosen_cell, PCAP, drawn).astype(jnp.int32)


def levels(own_key, dims, pieces, low, high):
    def one(position, blocks):
        heights = jax.random.uniform(jax.random.fold_in(jax.random.fold_in(own_key, 6), position), (blocks,), jnp.float32, low / len(pieces), high / len(pieces))
        return jnp.repeat(jnp.exp(heights), dims[position] // blocks).reshape((-1,) + (1,) * (len(dims) - position - 1))

    level = one(*pieces[0])
    for cut in pieces[1:]:
        level = level * one(*cut)
    return level


def normal_values(rng, extent, scale, most, pieces=(), kind=jnp.bfloat16):
    array = scale * jax.random.normal(rng, extent, jnp.float32)
    if pieces:
        array = array * levels(rng, extent, pieces, -0.22, 0.18)
    return jnp.clip(array, -most, most).astype(kind)


def setup_inputs(seed: int = 0) -> dict:
    key_list = jax.random.split(jax.random.key(seed), 6)
    return {
        "region_factors": normal_values(key_list[0], (REGIONS, RANK), (RANK ** -0.25), 1.25, ((0, 256),)),
        "item_factors": normal_values(key_list[1], (PANELS, BLOCK, RANK), (RANK ** -0.25), 1.25, ((0, 32), (1, 8))),
        "slab_blocks": normal_values(key_list[2], (DEVICES, PANELS, PCAP, BLOCK, BLOCK), 1.0, 6.0, ((0, 256),)),
        "block_rows": draw_block_rows(jax.random.fold_in(key_list[5], 71), 0),
        "counts": draw_counts(jax.random.fold_in(key_list[5], 71), 0),
    }


region_rate = 0.05
item_rate = 0.01
decay_rate = 0.1


def reference(region_factors, item_factors, slab_blocks, block_rows, counts):
    items_wide = item_factors.astype(jnp.float32)
    slot_ids = jnp.arange(PCAP, dtype=jnp.int32)
    block_ids = jnp.arange(RB_DEV, dtype=jnp.int32)
    region_blocks = region_factors.reshape(DEVICES, RB_DEV, BLOCK, RANK)

    def per_device(carried, inputs):
        device_rows, device_tiles, device_lists, device_counts = inputs
        present = slot_ids[None, :] < device_counts[:, None]
        chosen = device_rows[device_lists].astype(jnp.float32)
        predicted = jnp.einsum("psik,pjk->psij", chosen, items_wide)
        residual = jnp.where(present[:, :, None, None], predicted - device_tiles.astype(jnp.float32), 0.0)
        residual = residual.astype(jnp.bfloat16).astype(jnp.float32)
        terms = jnp.einsum("psij,pjk->psik", residual, items_wide)
        selector = (device_lists[:, :, None] == block_ids[None, None, :]).astype(jnp.float32)
        region_part = jnp.einsum("psr,psik->rik", selector, terms)
        carried = carried + jnp.einsum("psij,psik->pjk", residual, chosen)
        return carried, region_part

    item_grad, region_grad = lax.scan(
        per_device,
        jnp.zeros((PANELS, BLOCK, RANK), jnp.float32),
        (region_blocks, slab_blocks, block_rows, counts),
    )
    region_grad = region_grad.reshape(REGIONS, RANK)
    regions_wide = region_factors.astype(jnp.float32)
    new_regions = regions_wide - region_rate * (region_grad + decay_rate * regions_wide)
    new_items = items_wide - item_rate * (item_grad + decay_rate * items_wide)
    return new_regions, new_items
```

```python
import functools

import jax
import jax.numpy as jnp
from jax import lax
from jax.experimental import pallas as pl
from jax.experimental.pallas import tpu as pltpu
from jax.sharding import PartitionSpec as P

region_rate = 0.05
item_rate = 0.01
decay_rate = 0.1

PANELS_PER_STEP = 4


def grad_kernel(rows_ref, counts_ref, u_ref, v_ref, slab_ref, region_ref, item_ref):
    step = pl.program_id(0)
    group = v_ref.shape[0]
    slots = slab_ref.shape[1]

    @pl.when(step == 0)
    def _():
        region_ref[...] = jnp.zeros_like(region_ref)

    for g in range(group):
        panel = step * group + g
        count = counts_ref[panel]
        v = v_ref[g]
        for s in range(slots):
            def slot_work(s=s, g=g, v=v, panel=panel):
                b = rows_ref[panel * slots + s]
                u = u_ref[b]
                predicted = lax.dot_general(
                    u, v, (((1,), (1,)), ((), ())), preferred_element_type=jnp.float32
                )
                residual = (predicted - slab_ref[g, s].astype(jnp.float32)).astype(jnp.bfloat16)
                region_ref[b] += jnp.dot(residual, v, preferred_element_type=jnp.float32)
                term = lax.dot_general(
                    residual, u, (((0,), (0,)), ((), ())), preferred_element_type=jnp.float32
                )
                if s == 0:
                    item_ref[g] = term
                else:
                    item_ref[g] += term

            if s == 0:
                slot_work()
            else:
                pl.when(s < count)(slot_work)

    @pl.when(step == pl.num_programs(0) - 1)
    def _():
        wide = u_ref[...].astype(jnp.float32)
        region_ref[...] = wide - region_rate * (region_ref[...] + decay_rate * wide)


def local_grads(region_blocks, panels, tiles, rows_flat, counts):
    row_blocks, block, width = region_blocks.shape
    n_panels, slots = tiles.shape[0], tiles.shape[1]
    group = PANELS_PER_STEP
    grid_spec = pltpu.PrefetchScalarGridSpec(
        num_scalar_prefetch=2,
        grid=(n_panels // group,),
        in_specs=[
            pl.BlockSpec((row_blocks, block, width), lambda i, r, c: (0, 0, 0)),
            pl.BlockSpec((group, block, width), lambda i, r, c: (i, 0, 0)),
            pl.BlockSpec((group, slots, block, block), lambda i, r, c: (i, 0, 0, 0)),
        ],
        out_specs=[
            pl.BlockSpec((row_blocks, block, width), lambda i, r, c: (0, 0, 0)),
            pl.BlockSpec((group, block, width), lambda i, r, c: (i, 0, 0)),
        ],
    )
    flops = 3 * 2 * n_panels * slots * block * block * width
    bytes_accessed = (
        region_blocks.size * 2 + panels.size * 2 + tiles.size * 2
        + region_blocks.size * 4 + panels.size * 4
    )
    return pl.pallas_call(
        grad_kernel,
        grid_spec=grid_spec,
        out_shape=[
            jax.ShapeDtypeStruct((row_blocks, block, width), jnp.float32),
            jax.ShapeDtypeStruct((n_panels, block, width), jnp.float32),
        ],
        compiler_params=pltpu.CompilerParams(
            dimension_semantics=("arbitrary",),
            vmem_limit_bytes=48 * 1024 * 1024,
        ),
        cost_estimate=pl.CostEstimate(
            flops=flops, bytes_accessed=bytes_accessed, transcendentals=0
        ),
    )(rows_flat, counts, region_blocks, panels, tiles)


def on_device(region_factors, item_factors, slab_blocks, block_rows, counts):
    block = slab_blocks.shape[-1]
    width = region_factors.shape[-1]
    row_blocks = region_factors.shape[0] // block
    n_panels = slab_blocks.shape[1]
    region_blocks = region_factors.reshape(row_blocks, block, width)
    panel_own = lax.all_gather(item_factors, "row", axis=1, tiled=True)
    panels = lax.all_gather(panel_own, "col", axis=0, tiled=True)
    new_regions, item_part = local_grads(
        region_blocks, panels, slab_blocks[0], block_rows[0].reshape(-1), counts[0]
    )
    pieces = lax.axis_size("row")
    piece = block // pieces
    item_part = item_part.reshape(n_panels * pieces, piece, width)
    own_grad = lax.psum_scatter(item_part, ("col", "row"), scatter_dimension=0, tiled=True)
    own_rows = item_factors.astype(jnp.float32)
    new_items = own_rows - item_rate * (own_grad + decay_rate * own_rows)
    return (new_regions.reshape(row_blocks * block, width), new_items)


def solution(mesh):
    return jax.shard_map(
        on_device,
        mesh=mesh,
        in_specs=(
            P(("row", "col"), None),
            P("col", "row", None),
            P(("row", "col"), None, None, None, None),
            P(("row", "col"), None, None),
            P(("row", "col"), None),
        ),
        out_specs=(P(("row", "col"), None), P("col", "row", None)),
        check_vma=False,
    )
```

```python
import jax
import jax.numpy as jnp
from jax import lax
from jax.experimental import pallas as pl
from jax.experimental.pallas import tpu as pltpu
from jax.sharding import Mesh
from jax.sharding import PartitionSpec as P

region_rate = 0.05
item_rate = 0.01
decay_rate = 0.1

AXES = ("zh", "x", "zl", "y", "core")
Z_RING = ("zh", "zl")


def grad_kernel(rows_ref, counts_ref, u_ref, v_ref, slab_ref, region_ref, item_ref):
    step = pl.program_id(0)
    group = slab_ref.shape[0]
    slots = slab_ref.shape[1]

    @pl.when(step == 0)
    def _():
        region_ref[...] = jnp.zeros_like(region_ref)

    for g in range(group):
        panel = step * group + g
        count = counts_ref[panel]
        v = v_ref[g, 0, 0]
        for s in range(slots):
            def slot_work(s=s, g=g, v=v, panel=panel):
                b = rows_ref[panel * slots + s]
                u = u_ref[b]
                predicted = lax.dot_general(
                    u, v, (((1,), (1,)), ((), ())), preferred_element_type=jnp.float32
                )
                residual = (predicted - slab_ref[g, s].astype(jnp.float32)).astype(jnp.bfloat16)
                region_ref[b] += jnp.dot(residual, v, preferred_element_type=jnp.float32)
                term = lax.dot_general(
                    residual, u, (((0,), (0,)), ((), ())), preferred_element_type=jnp.float32
                )
                if s == 0:
                    item_ref[g, 0] = term
                else:
                    item_ref[g, 0] += term

            if s == 0:
                slot_work()
            else:
                pl.when(s < count)(slot_work)

    @pl.when(step == pl.num_programs(0) - 1)
    def _():
        wide = u_ref[...].astype(jnp.float32)
        region_ref[...] = wide - region_rate * (region_ref[...] + decay_rate * wide)


def local_grads(region_blocks, panels, tiles, rows_flat, counts):
    row_blocks, block, width = region_blocks.shape
    cores, ny, nzl = panels.shape[:3]
    n_panels, slots = tiles.shape[0], tiles.shape[1]
    grid_spec = pltpu.PrefetchScalarGridSpec(
        num_scalar_prefetch=2,
        grid=(n_panels // cores,),
        in_specs=[
            pl.BlockSpec((row_blocks, block, width), lambda i, r, c: (0, 0, 0)),
            pl.BlockSpec(
                (cores, 1, 1, block, width), lambda i, r, c: (0, i % ny, i // ny, 0, 0)
            ),
            pl.BlockSpec((cores, slots, block, block), lambda i, r, c: (i, 0, 0, 0)),
        ],
        out_specs=[
            pl.BlockSpec((row_blocks, block, width), lambda i, r, c: (0, 0, 0)),
            pl.BlockSpec(
                (cores, 1, block, width), lambda i, r, c: (0, (i % ny) * nzl + i // ny, 0, 0)
            ),
        ],
    )
    flops = 3 * 2 * n_panels * slots * block * block * width
    bytes_accessed = (
        region_blocks.size * 2 + panels.size * 2 + tiles.size * 2
        + region_blocks.size * 4 + panels.size * 4
    )
    return pl.pallas_call(
        grad_kernel,
        grid_spec=grid_spec,
        out_shape=[
            jax.ShapeDtypeStruct((row_blocks, block, width), jnp.float32),
            jax.ShapeDtypeStruct((cores, ny * nzl, block, width), jnp.float32),
        ],
        compiler_params=pltpu.CompilerParams(
            dimension_semantics=("arbitrary",),
            vmem_limit_bytes=48 * 1024 * 1024,
        ),
        cost_estimate=pl.CostEstimate(
            flops=flops, bytes_accessed=bytes_accessed, transcendentals=0
        ),
    )(rows_flat, counts, region_blocks, panels, tiles)


def take(arr, index):
    return lax.dynamic_index_in_dim(arr, index, 0, keepdims=False)


def ring_pairs(n, step):
    return [(s, (s + step) % n) for s in range(n)]


def ring_reduce_scatter(x, axes, n):
    me = lax.axis_index(axes)
    if n == 2:
        got = lax.ppermute(take(x, 1 - me), axes, ring_pairs(2, 1))
        return take(x, me) + got
    half = x.shape[1] // 2
    ahead, behind = x[:, :half], x[:, half:]
    acc_a = take(ahead, (me - 1) % n)
    acc_b = take(behind, (me + 1) % n)
    for t in range(n - 1):
        got_a = lax.ppermute(acc_a, axes, ring_pairs(n, 1))
        got_b = lax.ppermute(acc_b, axes, ring_pairs(n, n - 1))
        acc_a = got_a + take(ahead, (me - 2 - t) % n)
        acc_b = got_b + take(behind, (me + 2 + t) % n)
    return jnp.concatenate([acc_a, acc_b], axis=0)


def ring_all_gather(x, axes, n):
    me = lax.axis_index(axes)
    if n == 2:
        got = lax.ppermute(x, axes, ring_pairs(2, 1))
        out = jnp.zeros((2,) + x.shape, x.dtype)
        out = lax.dynamic_update_index_in_dim(out, x, me, 0)
        return lax.dynamic_update_index_in_dim(out, got, 1 - me, 0)
    half = x.shape[0] // 2
    cur_a, cur_b = x[:half], x[half:]
    buf_a = lax.dynamic_update_index_in_dim(
        jnp.zeros((n,) + cur_a.shape, x.dtype), cur_a, me, 0
    )
    buf_b = lax.dynamic_update_index_in_dim(
        jnp.zeros((n,) + cur_b.shape, x.dtype), cur_b, me, 0
    )
    for t in range(n - 1):
        cur_a = lax.ppermute(cur_a, axes, ring_pairs(n, 1))
        cur_b = lax.ppermute(cur_b, axes, ring_pairs(n, n - 1))
        buf_a = lax.dynamic_update_index_in_dim(buf_a, cur_a, (me - 1 - t) % n, 0)
        buf_b = lax.dynamic_update_index_in_dim(buf_b, cur_b, (me + 1 + t) % n, 0)
    return jnp.concatenate([buf_a, buf_b], axis=1)


def on_device(region_factors, item_factors, slab_blocks, block_rows, counts):
    n_zh, n_x = lax.axis_size("zh"), lax.axis_size("x")
    n_zl, n_y, n_core = lax.axis_size("zl"), lax.axis_size("y"), lax.axis_size("core")
    n_z = n_zh * n_zl
    block = slab_blocks.shape[-1]
    width = region_factors.shape[-1]
    row_blocks = region_factors.shape[0] // block
    region_blocks = region_factors.reshape(row_blocks, block, width)

    piece = item_factors[0]
    rows_x = ring_all_gather(piece, "x", n_x).reshape(-1, width)
    rows_z = ring_all_gather(rows_x, Z_RING, n_z)
    rows_z = rows_z.reshape(n_zh, n_zl, -1, width).transpose(1, 0, 2, 3)
    panel_z = rows_z.reshape(n_zl, block, width)
    panel_y = ring_all_gather(panel_z, "y", n_y)
    panels = ring_all_gather(panel_y, "core", n_core)

    new_regions, item_part = local_grads(
        region_blocks, panels, slab_blocks[0], block_rows[0].reshape(-1), counts[0]
    )

    grad_c = ring_reduce_scatter(item_part, "core", n_core)
    grad_c = grad_c.reshape(n_y, n_zl, block, width)
    grad_y = ring_reduce_scatter(grad_c, "y", n_y)
    grad_y = grad_y.reshape(n_zl, n_zh, -1, width).transpose(1, 0, 2, 3)
    grad_y = grad_y.reshape(n_z, -1, width)
    grad_z = ring_reduce_scatter(grad_y, Z_RING, n_z)
    grad_z = grad_z.reshape(n_x, -1, width)
    own_grad = ring_reduce_scatter(grad_z, "x", n_x)

    own_rows = piece.astype(jnp.float32)
    new_items = own_rows - item_rate * (own_grad + decay_rate * own_rows)
    return (new_regions.reshape(row_blocks * block, width), new_items[None])


def solution(mesh):
    rows, cols = mesh.devices.shape
    n_zh = 2
    n_core = 2
    n_x = rows // n_zh
    n_y = 4
    n_zl = cols // (n_y * n_core)
    fine = Mesh(mesh.devices.reshape(n_zh, n_x, n_zl, n_y, n_core), AXES)
    return jax.shard_map(
        on_device,
        mesh=fine,
        in_specs=(
            P(AXES, None),
            P(("zl", "y", "core"), ("zh", "x"), None),
            P(AXES, None, None, None, None),
            P(AXES, None, None),
            P(AXES, None),
        ),
        out_specs=(P(AXES, None), P(("zl", "y", "core"), ("zh", "x"), None)),
        check_vma=False,
    )
```

```python
import jax
import jax.numpy as jnp
from jax import lax
from jax.experimental import pallas as pl
from jax.experimental.pallas import tpu as pltpu
from jax.sharding import Mesh
from jax.sharding import PartitionSpec as P

region_rate = 0.05
item_rate = 0.01
decay_rate = 0.1

AXES = ("zh", "x", "zl", "y", "core")
Z_RING = ("zh", "zl")


def grad_kernel(rows_ref, counts_ref, u_ref, v_ref, slab_ref, region_ref, item_ref):
    step = pl.program_id(0)
    group = slab_ref.shape[0]
    slots = slab_ref.shape[1]

    @pl.when(step == 0)
    def _():
        region_ref[...] = jnp.zeros_like(region_ref)

    for g in range(group):
        panel = step * group + g
        count = counts_ref[panel]
        v = v_ref[g, 0, 0]
        for s in range(slots):
            def slot_work(s=s, g=g, v=v, panel=panel):
                b = rows_ref[panel * slots + s]
                u = u_ref[b]
                predicted = lax.dot_general(
                    u, v, (((1,), (1,)), ((), ())), preferred_element_type=jnp.float32
                )
                residual = (predicted - slab_ref[g, s].astype(jnp.float32)).astype(jnp.bfloat16)
                region_ref[b] += jnp.dot(residual, v, preferred_element_type=jnp.float32)
                term = lax.dot_general(
                    residual, u, (((0,), (0,)), ((), ())), preferred_element_type=jnp.float32
                )
                if s == 0:
                    item_ref[g, 0] = term
                else:
                    item_ref[g, 0] += term

            if s == 0:
                slot_work()
            else:
                pl.when(s < count)(slot_work)

    @pl.when(step == pl.num_programs(0) - 1)
    def _():
        wide = u_ref[...].astype(jnp.float32)
        region_ref[...] = wide - region_rate * (region_ref[...] + decay_rate * wide)


def local_grads(region_blocks, panels, tiles, rows_flat, counts):
    row_blocks, block, width = region_blocks.shape
    cores, ny, nzl = panels.shape[:3]
    n_panels, slots = tiles.shape[0], tiles.shape[1]
    grid_spec = pltpu.PrefetchScalarGridSpec(
        num_scalar_prefetch=2,
        grid=(n_panels // cores,),
        in_specs=[
            pl.BlockSpec((row_blocks, block, width), lambda i, r, c: (0, 0, 0)),
            pl.BlockSpec(
                (cores, 1, 1, block, width), lambda i, r, c: (0, i % ny, i // ny, 0, 0)
            ),
            pl.BlockSpec((cores, slots, block, block), lambda i, r, c: (i, 0, 0, 0)),
        ],
        out_specs=[
            pl.BlockSpec((row_blocks, block, width), lambda i, r, c: (0, 0, 0)),
            pl.BlockSpec(
                (cores, 1, block, width), lambda i, r, c: (0, (i % ny) * nzl + i // ny, 0, 0)
            ),
        ],
    )
    flops = 3 * 2 * n_panels * slots * block * block * width
    bytes_accessed = (
        region_blocks.size * 2 + panels.size * 2 + tiles.size * 2
        + region_blocks.size * 4 + panels.size * 4
    )
    return pl.pallas_call(
        grad_kernel,
        grid_spec=grid_spec,
        out_shape=[
            jax.ShapeDtypeStruct((row_blocks, block, width), jnp.float32),
            jax.ShapeDtypeStruct((cores, ny * nzl, block, width), jnp.float32),
        ],
        compiler_params=pltpu.CompilerParams(
            dimension_semantics=("arbitrary",),
            vmem_limit_bytes=48 * 1024 * 1024,
        ),
        cost_estimate=pl.CostEstimate(
            flops=flops, bytes_accessed=bytes_accessed, transcendentals=0
        ),
    )(rows_flat, counts, region_blocks, panels, tiles)


def take(arr, index):
    return lax.dynamic_index_in_dim(arr, index, 0, keepdims=False)


def put(arr, value, index):
    return lax.dynamic_update_index_in_dim(arr, value, index, 0)


def ring_pairs(n, step):
    return [(s, (s + step) % n) for s in range(n)]


def rings_reduce_scatter(jobs):
    state = []
    for x, axes, n in jobs:
        me = lax.axis_index(axes)
        half = x.shape[1] // 2
        ahead, behind = x[:, :half], x[:, half:]
        state.append([ahead, behind, axes, n, me, take(ahead, (me - 1) % n), take(behind, (me + 1) % n)])
    for t in range(max(job[2] for job in jobs) - 1):
        for st in state:
            ahead, behind, axes, n, me, acc_a, acc_b = st
            if t >= n - 1:
                continue
            got_a = lax.ppermute(acc_a, axes, ring_pairs(n, 1))
            got_b = lax.ppermute(acc_b, axes, ring_pairs(n, n - 1))
            st[5] = got_a + take(ahead, (me - 2 - t) % n)
            st[6] = got_b + take(behind, (me + 2 + t) % n)
    return [jnp.concatenate([st[5], st[6]], axis=0) for st in state]


def rings_all_gather(jobs):
    state = []
    for x, axes, n in jobs:
        me = lax.axis_index(axes)
        half = x.shape[0] // 2
        cur_a, cur_b = x[:half], x[half:]
        buf_a = put(jnp.zeros((n,) + cur_a.shape, x.dtype), cur_a, me)
        buf_b = put(jnp.zeros((n,) + cur_b.shape, x.dtype), cur_b, me)
        state.append([axes, n, me, cur_a, cur_b, buf_a, buf_b])
    for t in range(max(job[2] for job in jobs) - 1):
        for st in state:
            axes, n, me, cur_a, cur_b, buf_a, buf_b = st
            if t >= n - 1:
                continue
            cur_a = lax.ppermute(cur_a, axes, ring_pairs(n, 1))
            cur_b = lax.ppermute(cur_b, axes, ring_pairs(n, n - 1))
            st[3], st[4] = cur_a, cur_b
            st[5] = put(buf_a, cur_a, (me - 1 - t) % n)
            st[6] = put(buf_b, cur_b, (me + 1 + t) % n)
    return [jnp.concatenate([st[5], st[6]], axis=1) for st in state]


def direct_reduce_scatter(jobs):
    outs = []
    for x, axes, n in jobs:
        me = lax.axis_index(axes)
        total = take(x, me)
        for k in range(1, n):
            total = total + lax.ppermute(take(x, (me + k) % n), axes, ring_pairs(n, k))
        outs.append(total)
    return outs


def direct_all_gather(jobs):
    outs = []
    for x, axes, n in jobs:
        me = lax.axis_index(axes)
        buf = put(jnp.zeros((n,) + x.shape, x.dtype), x, me)
        for k in range(1, n):
            buf = put(buf, lax.ppermute(x, axes, ring_pairs(n, k)), (me - k) % n)
        outs.append(buf)
    return outs


def on_device(region_factors, item_factors, slab_blocks, block_rows, counts):
    n_zh, n_x = lax.axis_size("zh"), lax.axis_size("x")
    n_zl, n_y, n_core = lax.axis_size("zl"), lax.axis_size("y"), lax.axis_size("core")
    block = slab_blocks.shape[-1]
    width = region_factors.shape[-1]
    jj = block // (n_zh * n_x)
    hw = width // 2
    row_blocks = region_factors.shape[0] // block
    region_blocks = region_factors.reshape(row_blocks, block, width)

    piece = item_factors[0]
    (got,) = direct_all_gather([(piece, "zh", n_zh)])
    (got,) = direct_all_gather([(got, "zl", n_zl)])
    part_a, part_b = direct_all_gather([(got[..., :hw], "x", n_x), (got[..., hw:], "y", n_y)])
    part_a, part_b = rings_all_gather([(part_a, "y", n_y), (part_b, "x", n_x)])
    part_a = part_a.transpose(0, 2, 3, 1, 4, 5)
    part_b = part_b.transpose(1, 2, 3, 0, 4, 5)
    panel_y = jnp.concatenate([part_a, part_b], axis=-1).reshape(n_y, n_zl, block, width)
    (panels,) = direct_all_gather([(panel_y, "core", n_core)])

    new_regions, item_part = local_grads(
        region_blocks, panels, slab_blocks[0], block_rows[0].reshape(-1), counts[0]
    )

    (grad,) = direct_reduce_scatter([(item_part, "core", n_core)])
    grad = grad.reshape(n_y, n_zl, n_zh, n_x, jj, width)
    part_a = grad[..., :hw]
    part_b = grad[..., hw:].transpose(3, 0, 1, 2, 4, 5)
    part_a, part_b = rings_reduce_scatter([(part_a, "y", n_y), (part_b, "x", n_x)])
    part_a = part_a.transpose(2, 0, 1, 3, 4)
    part_a, part_b = direct_reduce_scatter([(part_a, "x", n_x), (part_b, "y", n_y)])
    grad = jnp.concatenate([part_a, part_b], axis=-1)
    (grad,) = direct_reduce_scatter([(grad, "zl", n_zl)])
    (own_grad,) = direct_reduce_scatter([(grad, "zh", n_zh)])

    own_rows = piece.astype(jnp.float32)
    new_items = own_rows - item_rate * (own_grad + decay_rate * own_rows)
    return (new_regions.reshape(row_blocks * block, width), new_items[None])


def solution(mesh):
    rows, cols = mesh.devices.shape
    n_zh = 2
    n_core = 2
    n_x = rows // n_zh
    n_y = 4
    n_zl = cols // (n_y * n_core)
    fine = Mesh(mesh.devices.reshape(n_zh, n_x, n_zl, n_y, n_core), AXES)
    return jax.shard_map(
        on_device,
        mesh=fine,
        in_specs=(
            P(AXES, None),
            P(("zl", "y", "core"), ("zh", "x"), None),
            P(AXES, None, None, None, None),
            P(AXES, None, None),
            P(AXES, None),
        ),
        out_specs=(P(AXES, None), P(("zl", "y", "core"), ("zh", "x"), None)),
        check_vma=False,
    )
```

```python
import jax
import jax.numpy as jnp
from jax import lax
from jax.experimental import pallas as pl
from jax.experimental.pallas import tpu as pltpu
from jax.sharding import Mesh
from jax.sharding import PartitionSpec as P

region_rate = 0.05
item_rate = 0.01
decay_rate = 0.1

AXES = ("zh", "x", "zl", "y", "core")
Z_RING = ("zh", "zl")


def grad_kernel(rows_ref, counts_ref, u_ref, v_ref, slab_ref, region_ref, item_ref):
    step = pl.program_id(0)
    group = slab_ref.shape[0]
    slots, block = slab_ref.shape[1], slab_ref.shape[2]

    @pl.when(step == 0)
    def _():
        region_ref[...] = jnp.zeros_like(region_ref)

    for g in range(group):
        panel = step * group + g
        count = counts_ref[panel]
        v = v_ref[g, 0, 0]
        chosen_rows = [rows_ref[panel * slots + s] for s in range(slots)]
        chosen = jnp.concatenate([u_ref[b] for b in chosen_rows], axis=0)
        predicted = lax.dot_general(
            chosen, v, (((1,), (1,)), ((), ())), preferred_element_type=jnp.float32
        )
        tiles = slab_ref[g].reshape(slots * block, block).astype(jnp.float32)
        slot_of = lax.broadcasted_iota(jnp.int32, (slots * block, block), 0) // block
        residual = jnp.where(slot_of < count, predicted - tiles, 0.0).astype(jnp.bfloat16)
        item_ref[g, 0] = lax.dot_general(
            residual, chosen, (((0,), (0,)), ((), ())), preferred_element_type=jnp.float32
        )
        terms = jnp.dot(residual, v, preferred_element_type=jnp.float32)
        for s, b in enumerate(chosen_rows):
            region_ref[b] += terms[s * block:(s + 1) * block]

    @pl.when(step == pl.num_programs(0) - 1)
    def _():
        wide = u_ref[...].astype(jnp.float32)
        region_ref[...] = wide - region_rate * (region_ref[...] + decay_rate * wide)


def local_grads(region_blocks, panels, tiles, rows_flat, counts):
    row_blocks, block, width = region_blocks.shape
    cores, ny, nzl = panels.shape[:3]
    n_panels, slots = tiles.shape[0], tiles.shape[1]
    grid_spec = pltpu.PrefetchScalarGridSpec(
        num_scalar_prefetch=2,
        grid=(n_panels // cores,),
        in_specs=[
            pl.BlockSpec((row_blocks, block, width), lambda i, r, c: (0, 0, 0)),
            pl.BlockSpec(
                (cores, 1, 1, block, width), lambda i, r, c: (0, i % ny, i // ny, 0, 0)
            ),
            pl.BlockSpec((cores, slots, block, block), lambda i, r, c: (i, 0, 0, 0)),
        ],
        out_specs=[
            pl.BlockSpec((row_blocks, block, width), lambda i, r, c: (0, 0, 0)),
            pl.BlockSpec(
                (cores, 1, block, width), lambda i, r, c: (0, (i % ny) * nzl + i // ny, 0, 0)
            ),
        ],
    )
    flops = 3 * 2 * n_panels * slots * block * block * width
    bytes_accessed = (
        region_blocks.size * 2 + panels.size * 2 + tiles.size * 2
        + region_blocks.size * 4 + panels.size * 4
    )
    return pl.pallas_call(
        grad_kernel,
        grid_spec=grid_spec,
        out_shape=[
            jax.ShapeDtypeStruct((row_blocks, block, width), jnp.float32),
            jax.ShapeDtypeStruct((cores, ny * nzl, block, width), jnp.float32),
        ],
        compiler_params=pltpu.CompilerParams(
            dimension_semantics=("arbitrary",),
            vmem_limit_bytes=48 * 1024 * 1024,
        ),
        cost_estimate=pl.CostEstimate(
            flops=flops, bytes_accessed=bytes_accessed, transcendentals=0
        ),
    )(rows_flat, counts, region_blocks, panels, tiles)


def take(arr, index):
    return lax.dynamic_index_in_dim(arr, index, 0, keepdims=False)


def put(arr, value, index):
    return lax.dynamic_update_index_in_dim(arr, value, index, 0)


def ring_pairs(n, step):
    return [(s, (s + step) % n) for s in range(n)]


def rings_reduce_scatter(jobs):
    state = []
    for x, axes, n in jobs:
        me = lax.axis_index(axes)
        half = x.shape[1] // 2
        ahead, behind = x[:, :half], x[:, half:]
        state.append([ahead, behind, axes, n, me, take(ahead, (me - 1) % n), take(behind, (me + 1) % n)])
    for t in range(max(job[2] for job in jobs) - 1):
        for st in state:
            ahead, behind, axes, n, me, acc_a, acc_b = st
            if t >= n - 1:
                continue
            got_a = lax.ppermute(acc_a, axes, ring_pairs(n, 1))
            got_b = lax.ppermute(acc_b, axes, ring_pairs(n, n - 1))
            st[5] = got_a + take(ahead, (me - 2 - t) % n)
            st[6] = got_b + take(behind, (me + 2 + t) % n)
    return [jnp.concatenate([st[5], st[6]], axis=0) for st in state]


def rings_all_gather(jobs):
    state = []
    for x, axes, n in jobs:
        me = lax.axis_index(axes)
        half = x.shape[0] // 2
        cur_a, cur_b = x[:half], x[half:]
        buf_a = put(jnp.zeros((n,) + cur_a.shape, x.dtype), cur_a, me)
        buf_b = put(jnp.zeros((n,) + cur_b.shape, x.dtype), cur_b, me)
        state.append([axes, n, me, cur_a, cur_b, buf_a, buf_b])
    for t in range(max(job[2] for job in jobs) - 1):
        for st in state:
            axes, n, me, cur_a, cur_b, buf_a, buf_b = st
            if t >= n - 1:
                continue
            cur_a = lax.ppermute(cur_a, axes, ring_pairs(n, 1))
            cur_b = lax.ppermute(cur_b, axes, ring_pairs(n, n - 1))
            st[3], st[4] = cur_a, cur_b
            st[5] = put(buf_a, cur_a, (me - 1 - t) % n)
            st[6] = put(buf_b, cur_b, (me + 1 + t) % n)
    return [jnp.concatenate([st[5], st[6]], axis=1) for st in state]


def direct_reduce_scatter(jobs):
    outs = []
    for x, axes, n in jobs:
        me = lax.axis_index(axes)
        total = take(x, me)
        for k in range(1, n):
            total = total + lax.ppermute(take(x, (me + k) % n), axes, ring_pairs(n, k))
        outs.append(total)
    return outs


def direct_all_gather(jobs):
    outs = []
    for x, axes, n in jobs:
        me = lax.axis_index(axes)
        buf = put(jnp.zeros((n,) + x.shape, x.dtype), x, me)
        for k in range(1, n):
            buf = put(buf, lax.ppermute(x, axes, ring_pairs(n, k)), (me - k) % n)
        outs.append(buf)
    return outs


def on_device(region_factors, item_factors, slab_blocks, block_rows, counts):
    n_zh, n_x = lax.axis_size("zh"), lax.axis_size("x")
    n_zl, n_y, n_core = lax.axis_size("zl"), lax.axis_size("y"), lax.axis_size("core")
    block = slab_blocks.shape[-1]
    width = region_factors.shape[-1]
    jj = block // (n_zh * n_x)
    hw = width // 2
    row_blocks = region_factors.shape[0] // block
    region_blocks = region_factors.reshape(row_blocks, block, width)

    piece = item_factors[0]
    (got,) = direct_all_gather([(piece, "zh", n_zh)])
    (got,) = direct_all_gather([(got, "zl", n_zl)])
    part_a, part_b = direct_all_gather([(got[..., :hw], "x", n_x), (got[..., hw:], "y", n_y)])
    part_a, part_b = rings_all_gather([(part_a, "y", n_y), (part_b, "x", n_x)])
    part_a = part_a.transpose(0, 2, 3, 1, 4, 5)
    part_b = part_b.transpose(1, 2, 3, 0, 4, 5)
    panel_y = jnp.concatenate([part_a, part_b], axis=-1).reshape(n_y, n_zl, block, width)
    (panels,) = direct_all_gather([(panel_y, "core", n_core)])

    new_regions, item_part = local_grads(
        region_blocks, panels, slab_blocks[0], block_rows[0].reshape(-1), counts[0]
    )

    (grad,) = direct_reduce_scatter([(item_part, "core", n_core)])
    grad = grad.reshape(n_y, n_zl, n_zh, n_x, jj, width)
    part_a = grad[..., :hw]
    part_b = grad[..., hw:].transpose(3, 0, 1, 2, 4, 5)
    part_a, part_b = rings_reduce_scatter([(part_a, "y", n_y), (part_b, "x", n_x)])
    part_a = part_a.transpose(2, 0, 1, 3, 4)
    part_a, part_b = direct_reduce_scatter([(part_a, "x", n_x), (part_b, "y", n_y)])
    grad = jnp.concatenate([part_a, part_b], axis=-1)
    (grad,) = direct_reduce_scatter([(grad, "zl", n_zl)])
    (own_grad,) = direct_reduce_scatter([(grad, "zh", n_zh)])

    own_rows = piece.astype(jnp.float32)
    new_items = own_rows - item_rate * (own_grad + decay_rate * own_rows)
    return (new_regions.reshape(row_blocks * block, width), new_items[None])


def solution(mesh):
    rows, cols = mesh.devices.shape
    n_zh = 2
    n_core = 2
    n_x = rows // n_zh
    n_y = 4
    n_zl = cols // (n_y * n_core)
    fine = Mesh(mesh.devices.reshape(n_zh, n_x, n_zl, n_y, n_core), AXES)
    return jax.shard_map(
        on_device,
        mesh=fine,
        in_specs=(
            P(AXES, None),
            P(("zl", "y", "core"), ("zh", "x"), None),
            P(AXES, None, None, None, None),
            P(AXES, None, None),
            P(AXES, None),
        ),
        out_specs=(P(AXES, None), P(("zl", "y", "core"), ("zh", "x"), None)),
        check_vma=False,
    )
```

```python
import functools

import jax
import jax.numpy as jnp
from jax import lax
from jax.experimental import pallas as pl
from jax.experimental.pallas import tpu as pltpu
from jax.sharding import Mesh
from jax.sharding import PartitionSpec as P

region_rate = 0.05
item_rate = 0.01
decay_rate = 0.1

AXES = ("zh", "x", "zl", "y", "core")
Z_RING = ("zh", "zl")


def grad_kernel(first, last, ny, rows_ref, counts_ref, sel_ref, u_ref, v_ref, slab0_ref, slab1_ref, *rest):
    if first:
        region_ref, item_ref = rest
    else:
        region_in_ref, region_ref, item_ref = rest
    step = pl.program_id(0)
    slots, block = slab0_ref.shape[1], slab0_ref.shape[2]
    pairs = ny // 2
    zl = step // pairs
    pair = step % pairs

    @pl.when(step == 0)
    def _():
        if first:
            region_ref[...] = jnp.zeros_like(region_ref)
        else:
            region_ref[...] = region_in_ref[...]

    for g, slab_ref in enumerate((slab0_ref, slab1_ref)):
        panel = (zl * ny + 2 * pair + g) * 2 + sel_ref[0]
        count = counts_ref[panel]
        v = v_ref[g, 0]
        chosen_rows = [rows_ref[panel * slots + s] for s in range(slots)]
        chosen = jnp.concatenate([u_ref[b] for b in chosen_rows], axis=0)
        predicted = lax.dot_general(
            chosen, v, (((1,), (1,)), ((), ())), preferred_element_type=jnp.float32
        )
        tiles = slab_ref[0].reshape(slots * block, block).astype(jnp.float32)
        slot_of = lax.broadcasted_iota(jnp.int32, (slots * block, block), 0) // block
        residual = jnp.where(slot_of < count, predicted - tiles, 0.0).astype(jnp.bfloat16)
        item_ref[g, 0] = lax.dot_general(
            residual, chosen, (((0,), (0,)), ((), ())), preferred_element_type=jnp.float32
        )
        terms = jnp.dot(residual, v, preferred_element_type=jnp.float32)
        for s, b in enumerate(chosen_rows):
            region_ref[b] += terms[s * block:(s + 1) * block]

    if last:
        @pl.when(step == pl.num_programs(0) - 1)
        def _():
            wide = u_ref[...].astype(jnp.float32)
            region_ref[...] = wide - region_rate * (region_ref[...] + decay_rate * wide)


def local_grads(region_blocks, panels, tiles, rows_flat, counts, core_sel, region_in, last):
    row_blocks, block, width = region_blocks.shape
    ny, nzl = panels.shape[:2]
    slots = tiles.shape[1]
    pairs = ny // 2
    first = region_in is None

    def slab_map(g):
        return lambda i, r, c, s: (((i // pairs) * ny + 2 * (i % pairs) + g) * 2 + s[0], 0, 0, 0)

    in_specs = [
        pl.BlockSpec((row_blocks, block, width), lambda i, r, c, s: (0, 0, 0)),
        pl.BlockSpec((2, 1, block, width), lambda i, r, c, s: (i % pairs, i // pairs, 0, 0)),
        pl.BlockSpec((1, slots, block, block), slab_map(0)),
        pl.BlockSpec((1, slots, block, block), slab_map(1)),
    ]
    operands = [region_blocks, panels, tiles, tiles]
    aliases = {}
    if not first:
        in_specs.append(pl.BlockSpec((row_blocks, block, width), lambda i, r, c, s: (0, 0, 0)))
        operands.append(region_in)
        aliases = {3 + len(operands) - 1: 0}
    grid_spec = pltpu.PrefetchScalarGridSpec(
        num_scalar_prefetch=3,
        grid=(ny * nzl // 2,),
        in_specs=in_specs,
        out_specs=[
            pl.BlockSpec((row_blocks, block, width), lambda i, r, c, s: (0, 0, 0)),
            pl.BlockSpec((2, 1, block, width), lambda i, r, c, s: (i % pairs, i // pairs, 0, 0)),
        ],
    )
    n_panels = ny * nzl
    flops = 3 * 2 * n_panels * slots * block * block * width
    bytes_accessed = (
        region_blocks.size * 2 + panels.size * 2 + n_panels * slots * block * block * 2
        + region_blocks.size * 8 + panels.size * 4
    )
    return pl.pallas_call(
        functools.partial(grad_kernel, first, last, ny),
        grid_spec=grid_spec,
        out_shape=[
            jax.ShapeDtypeStruct((row_blocks, block, width), jnp.float32),
            jax.ShapeDtypeStruct((ny, nzl, block, width), jnp.float32),
        ],
        input_output_aliases=aliases,
        compiler_params=pltpu.CompilerParams(
            dimension_semantics=("arbitrary",),
            vmem_limit_bytes=48 * 1024 * 1024,
        ),
        cost_estimate=pl.CostEstimate(
            flops=flops, bytes_accessed=bytes_accessed, transcendentals=0
        ),
    )(rows_flat, counts, core_sel, *operands)


def take(arr, index):
    return lax.dynamic_index_in_dim(arr, index, 0, keepdims=False)


def put(arr, value, index):
    return lax.dynamic_update_index_in_dim(arr, value, index, 0)


def ring_pairs(n, step):
    return [(s, (s + step) % n) for s in range(n)]


def rings_reduce_scatter(jobs):
    state = []
    for x, axes, n in jobs:
        me = lax.axis_index(axes)
        half = x.shape[1] // 2
        ahead, behind = x[:, :half], x[:, half:]
        state.append([ahead, behind, axes, n, me, take(ahead, (me - 1) % n), take(behind, (me + 1) % n)])
    for t in range(max(job[2] for job in jobs) - 1):
        for st in state:
            ahead, behind, axes, n, me, acc_a, acc_b = st
            if t >= n - 1:
                continue
            got_a = lax.ppermute(acc_a, axes, ring_pairs(n, 1))
            got_b = lax.ppermute(acc_b, axes, ring_pairs(n, n - 1))
            st[5] = got_a + take(ahead, (me - 2 - t) % n)
            st[6] = got_b + take(behind, (me + 2 + t) % n)
    return [jnp.concatenate([st[5], st[6]], axis=0) for st in state]


def rings_all_gather(jobs):
    state = []
    for x, axes, n in jobs:
        me = lax.axis_index(axes)
        half = x.shape[0] // 2
        cur_a, cur_b = x[:half], x[half:]
        buf_a = put(jnp.zeros((n,) + cur_a.shape, x.dtype), cur_a, me)
        buf_b = put(jnp.zeros((n,) + cur_b.shape, x.dtype), cur_b, me)
        state.append([axes, n, me, cur_a, cur_b, buf_a, buf_b])
    for t in range(max(job[2] for job in jobs) - 1):
        for st in state:
            axes, n, me, cur_a, cur_b, buf_a, buf_b = st
            if t >= n - 1:
                continue
            cur_a = lax.ppermute(cur_a, axes, ring_pairs(n, 1))
            cur_b = lax.ppermute(cur_b, axes, ring_pairs(n, n - 1))
            st[3], st[4] = cur_a, cur_b
            st[5] = put(buf_a, cur_a, (me - 1 - t) % n)
            st[6] = put(buf_b, cur_b, (me + 1 + t) % n)
    return [jnp.concatenate([st[5], st[6]], axis=1) for st in state]


def direct_reduce_scatter(jobs):
    outs = []
    for x, axes, n in jobs:
        me = lax.axis_index(axes)
        total = take(x, me)
        for k in range(1, n):
            total = total + lax.ppermute(take(x, (me + k) % n), axes, ring_pairs(n, k))
        outs.append(total)
    return outs


def direct_all_gather(jobs):
    outs = []
    for x, axes, n in jobs:
        me = lax.axis_index(axes)
        buf = put(jnp.zeros((n,) + x.shape, x.dtype), x, me)
        for k in range(1, n):
            buf = put(buf, lax.ppermute(x, axes, ring_pairs(n, k)), (me - k) % n)
        outs.append(buf)
    return outs


def on_device(region_factors, item_factors, slab_blocks, block_rows, counts):
    n_zh, n_x = lax.axis_size("zh"), lax.axis_size("x")
    n_zl, n_y, n_core = lax.axis_size("zl"), lax.axis_size("y"), lax.axis_size("core")
    block = slab_blocks.shape[-1]
    width = region_factors.shape[-1]
    jj = block // (n_zh * n_x)
    hw = width // 2
    row_blocks = region_factors.shape[0] // block
    region_blocks = region_factors.reshape(row_blocks, block, width)

    piece = item_factors[0]
    (got,) = direct_all_gather([(piece, "zh", n_zh)])
    (got,) = direct_all_gather([(got, "zl", n_zl)])
    part_a, part_b = direct_all_gather([(got[..., :hw], "x", n_x), (got[..., hw:], "y", n_y)])
    part_a, part_b = rings_all_gather([(part_a, "y", n_y), (part_b, "x", n_x)])
    part_a = part_a.transpose(0, 2, 3, 1, 4, 5)
    part_b = part_b.transpose(1, 2, 3, 0, 4, 5)
    panel_y = jnp.concatenate([part_a, part_b], axis=-1).reshape(n_y, n_zl, block, width)
    swap = ring_pairs(n_core, 1)
    panel_other = lax.ppermute(panel_y, "core", swap)

    me = lax.axis_index("core")
    tiles, rows_flat, live = slab_blocks[0], block_rows[0].reshape(-1), counts[0]
    partial_regions, other_part = local_grads(
        region_blocks, panel_other, tiles, rows_flat, live, (1 - me)[None], None, False
    )
    got = lax.ppermute(other_part, "core", swap)
    new_regions, own_part = local_grads(
        region_blocks, panel_y, tiles, rows_flat, live, me[None], partial_regions, True
    )

    grad = own_part + got
    grad = grad.reshape(n_y, n_zl, n_zh, n_x, jj, width)
    part_a = grad[..., :hw]
    part_b = grad[..., hw:].transpose(3, 0, 1, 2, 4, 5)
    part_a, part_b = rings_reduce_scatter([(part_a, "y", n_y), (part_b, "x", n_x)])
    part_a = part_a.transpose(2, 0, 1, 3, 4)
    part_a, part_b = direct_reduce_scatter([(part_a, "x", n_x), (part_b, "y", n_y)])
    grad = jnp.concatenate([part_a, part_b], axis=-1)
    (grad,) = direct_reduce_scatter([(grad, "zl", n_zl)])
    (own_grad,) = direct_reduce_scatter([(grad, "zh", n_zh)])

    own_rows = piece.astype(jnp.float32)
    new_items = own_rows - item_rate * (own_grad + decay_rate * own_rows)
    return (new_regions.reshape(row_blocks * block, width), new_items[None])


def solution(mesh):
    rows, cols = mesh.devices.shape
    n_zh = 2
    n_core = 2
    n_x = rows // n_zh
    n_y = 4
    n_zl = cols // (n_y * n_core)
    fine = Mesh(mesh.devices.reshape(n_zh, n_x, n_zl, n_y, n_core), AXES)
    return jax.shard_map(
        on_device,
        mesh=fine,
        in_specs=(
            P(AXES, None),
            P(("zl", "y", "core"), ("zh", "x"), None),
            P(AXES, None, None, None, None),
            P(AXES, None, None),
            P(AXES, None),
        ),
        out_specs=(P(AXES, None), P(("zl", "y", "core"), ("zh", "x"), None)),
        check_vma=False,
    )
```

```python
import functools

import jax
import jax.numpy as jnp
from jax import lax
from jax.experimental import pallas as pl
from jax.experimental.pallas import tpu as pltpu
from jax.sharding import Mesh
from jax.sharding import PartitionSpec as P

region_rate = 0.05
item_rate = 0.01
decay_rate = 0.1

AXES = ("zh", "x", "zl", "y", "core")
Z_RING = ("zh", "zl")


def grad_kernel(first, last, ny, rows_ref, counts_ref, sel_ref, u_ref, v_ref, slab0_ref, slab1_ref, *rest):
    if first:
        region_ref, item_ref = rest
    else:
        region_in_ref, region_ref, item_ref = rest
    step = pl.program_id(0)
    slots, block = slab0_ref.shape[1], slab0_ref.shape[2]
    pairs = ny // 2
    zl = step // pairs
    pair = step % pairs

    @pl.when(step == 0)
    def _():
        if first:
            region_ref[...] = jnp.zeros_like(region_ref)
        else:
            region_ref[...] = region_in_ref[...]

    for g, slab_ref in enumerate((slab0_ref, slab1_ref)):
        panel = (zl * ny + 2 * pair + g) * 2 + sel_ref[0]
        count = counts_ref[panel]
        v = v_ref[g, 0]
        chosen_rows = [rows_ref[panel * slots + s] for s in range(slots)]
        chosen = jnp.concatenate([u_ref[b] for b in chosen_rows], axis=0)
        predicted = lax.dot_general(
            chosen, v, (((1,), (1,)), ((), ())), preferred_element_type=jnp.float32
        )
        tiles = slab_ref[0].reshape(slots * block, block).astype(jnp.float32)
        slot_of = lax.broadcasted_iota(jnp.int32, (slots * block, block), 0) // block
        residual = jnp.where(slot_of < count, predicted - tiles, 0.0).astype(jnp.bfloat16)
        item_ref[g, 0] = lax.dot_general(
            residual, chosen, (((0,), (0,)), ((), ())), preferred_element_type=jnp.float32
        )
        terms = jnp.dot(residual, v, preferred_element_type=jnp.float32)
        for s, b in enumerate(chosen_rows):
            region_ref[b] += terms[s * block:(s + 1) * block]

    if last:
        @pl.when(step == pl.num_programs(0) - 1)
        def _():
            wide = u_ref[...].astype(jnp.float32)
            region_ref[...] = wide - region_rate * (region_ref[...] + decay_rate * wide)


def local_grads(region_blocks, panels, tiles, rows_flat, counts, core_sel, region_in, last):
    row_blocks, block, width = region_blocks.shape
    ny, nzl = panels.shape[:2]
    slots = tiles.shape[1]
    pairs = ny // 2
    first = region_in is None

    def slab_map(g):
        return lambda i, r, c, s: (((i // pairs) * ny + 2 * (i % pairs) + g) * 2 + s[0], 0, 0, 0)

    in_specs = [
        pl.BlockSpec((row_blocks, block, width), lambda i, r, c, s: (0, 0, 0)),
        pl.BlockSpec((2, 1, block, width), lambda i, r, c, s: (i % pairs, i // pairs, 0, 0)),
        pl.BlockSpec((1, slots, block, block), slab_map(0)),
        pl.BlockSpec((1, slots, block, block), slab_map(1)),
    ]
    operands = [region_blocks, panels, tiles, tiles]
    aliases = {}
    if not first:
        in_specs.append(pl.BlockSpec((row_blocks, block, width), lambda i, r, c, s: (0, 0, 0)))
        operands.append(region_in)
        aliases = {3 + len(operands) - 1: 0}
    grid_spec = pltpu.PrefetchScalarGridSpec(
        num_scalar_prefetch=3,
        grid=(ny * nzl // 2,),
        in_specs=in_specs,
        out_specs=[
            pl.BlockSpec((row_blocks, block, width), lambda i, r, c, s: (0, 0, 0)),
            pl.BlockSpec((2, 1, block, width), lambda i, r, c, s: (i % pairs, i // pairs, 0, 0)),
        ],
    )
    n_panels = ny * nzl
    flops = 3 * 2 * n_panels * slots * block * block * width
    bytes_accessed = (
        region_blocks.size * 2 + panels.size * 2 + n_panels * slots * block * block * 2
        + region_blocks.size * 8 + panels.size * 4
    )
    return pl.pallas_call(
        functools.partial(grad_kernel, first, last, ny),
        grid_spec=grid_spec,
        out_shape=[
            jax.ShapeDtypeStruct((row_blocks, block, width), jnp.float32),
            jax.ShapeDtypeStruct((ny, nzl, block, width), jnp.float32),
        ],
        input_output_aliases=aliases,
        compiler_params=pltpu.CompilerParams(
            dimension_semantics=("arbitrary",),
            vmem_limit_bytes=48 * 1024 * 1024,
        ),
        cost_estimate=pl.CostEstimate(
            flops=flops, bytes_accessed=bytes_accessed, transcendentals=0
        ),
    )(rows_flat, counts, core_sel, *operands)


def take(arr, index):
    return lax.dynamic_index_in_dim(arr, index, 0, keepdims=False)


def put(arr, value, index):
    return lax.dynamic_update_index_in_dim(arr, value, index, 0)


def ring_pairs(n, step):
    return [(s, (s + step) % n) for s in range(n)]


def rings_reduce_scatter(jobs):
    state = []
    for x, axes, n in jobs:
        me = lax.axis_index(axes)
        half = x.shape[1] // 2
        ahead, behind = x[:, :half], x[:, half:]
        state.append([ahead, behind, axes, n, me, take(ahead, (me - 1) % n), take(behind, (me + 1) % n)])
    for t in range(max(job[2] for job in jobs) - 1):
        for st in state:
            ahead, behind, axes, n, me, acc_a, acc_b = st
            if t >= n - 1:
                continue
            got_a = lax.ppermute(acc_a, axes, ring_pairs(n, 1))
            got_b = lax.ppermute(acc_b, axes, ring_pairs(n, n - 1))
            st[5] = got_a + take(ahead, (me - 2 - t) % n)
            st[6] = got_b + take(behind, (me + 2 + t) % n)
    return [jnp.concatenate([st[5], st[6]], axis=0) for st in state]


def rings_all_gather(jobs):
    state = []
    for x, axes, n in jobs:
        me = lax.axis_index(axes)
        half = x.shape[0] // 2
        cur_a, cur_b = x[:half], x[half:]
        buf_a = put(jnp.zeros((n,) + cur_a.shape, x.dtype), cur_a, me)
        buf_b = put(jnp.zeros((n,) + cur_b.shape, x.dtype), cur_b, me)
        state.append([axes, n, me, cur_a, cur_b, buf_a, buf_b])
    for t in range(max(job[2] for job in jobs) - 1):
        for st in state:
            axes, n, me, cur_a, cur_b, buf_a, buf_b = st
            if t >= n - 1:
                continue
            cur_a = lax.ppermute(cur_a, axes, ring_pairs(n, 1))
            cur_b = lax.ppermute(cur_b, axes, ring_pairs(n, n - 1))
            st[3], st[4] = cur_a, cur_b
            st[5] = put(buf_a, cur_a, (me - 1 - t) % n)
            st[6] = put(buf_b, cur_b, (me + 1 + t) % n)
    return [jnp.concatenate([st[5], st[6]], axis=1) for st in state]


def direct_reduce_scatter(jobs):
    outs = []
    for x, axes, n in jobs:
        me = lax.axis_index(axes)
        total = take(x, me)
        for k in range(1, n):
            total = total + lax.ppermute(take(x, (me + k) % n), axes, ring_pairs(n, k))
        outs.append(total)
    return outs


def direct_all_gather(jobs):
    outs = []
    for x, axes, n in jobs:
        me = lax.axis_index(axes)
        buf = put(jnp.zeros((n,) + x.shape, x.dtype), x, me)
        for k in range(1, n):
            buf = put(buf, lax.ppermute(x, axes, ring_pairs(n, k)), (me - k) % n)
        outs.append(buf)
    return outs


def on_device(region_factors, item_factors, slab_blocks, block_rows, counts):
    n_zh, n_x = lax.axis_size("zh"), lax.axis_size("x")
    n_zl, n_y, n_core = lax.axis_size("zl"), lax.axis_size("y"), lax.axis_size("core")
    block = slab_blocks.shape[-1]
    width = region_factors.shape[-1]
    jj = block // (n_zh * n_x)
    hw = width // 2
    row_blocks = region_factors.shape[0] // block
    region_blocks = region_factors.reshape(row_blocks, block, width)

    piece = item_factors[0]
    (got,) = direct_all_gather([(piece, "zh", n_zh)])
    (got,) = direct_all_gather([(got, "zl", n_zl)])
    part_a, part_b = direct_all_gather([(got[..., :hw], "x", n_x), (got[..., hw:], "y", n_y)])
    part_a, part_b = direct_all_gather([(part_a, "y", n_y), (part_b, "x", n_x)])
    part_a = part_a.transpose(0, 2, 3, 1, 4, 5)
    part_b = part_b.transpose(1, 2, 3, 0, 4, 5)
    panel_y = jnp.concatenate([part_a, part_b], axis=-1).reshape(n_y, n_zl, block, width)
    swap = ring_pairs(n_core, 1)
    panel_other = lax.ppermute(panel_y, "core", swap)

    me = lax.axis_index("core")
    tiles, rows_flat, live = slab_blocks[0], block_rows[0].reshape(-1), counts[0]
    partial_regions, other_part = local_grads(
        region_blocks, panel_other, tiles, rows_flat, live, (1 - me)[None], None, False
    )
    got = lax.ppermute(other_part, "core", swap)
    new_regions, own_part = local_grads(
        region_blocks, panel_y, tiles, rows_flat, live, me[None], partial_regions, True
    )

    grad = own_part + got
    grad = grad.reshape(n_y, n_zl, n_zh, n_x, jj, width)
    part_a = grad[..., :hw]
    part_b = grad[..., hw:].transpose(3, 0, 1, 2, 4, 5)
    part_a, part_b = rings_reduce_scatter([(part_a, "y", n_y), (part_b, "x", n_x)])
    part_a = part_a.transpose(2, 0, 1, 3, 4)
    part_a, part_b = direct_reduce_scatter([(part_a, "x", n_x), (part_b, "y", n_y)])
    grad = jnp.concatenate([part_a, part_b], axis=-1)
    (grad,) = direct_reduce_scatter([(grad, "zl", n_zl)])
    (own_grad,) = direct_reduce_scatter([(grad, "zh", n_zh)])

    own_rows = piece.astype(jnp.float32)
    new_items = own_rows - item_rate * (own_grad + decay_rate * own_rows)
    return (new_regions.reshape(row_blocks * block, width), new_items[None])


def solution(mesh):
    rows, cols = mesh.devices.shape
    n_zh = 2
    n_core = 2
    n_x = rows // n_zh
    n_y = 4
    n_zl = cols // (n_y * n_core)
    fine = Mesh(mesh.devices.reshape(n_zh, n_x, n_zl, n_y, n_core), AXES)
    return jax.shard_map(
        on_device,
        mesh=fine,
        in_specs=(
            P(AXES, None),
            P(("zl", "y", "core"), ("zh", "x"), None),
            P(AXES, None, None, None, None),
            P(AXES, None, None),
            P(AXES, None),
        ),
        out_specs=(P(AXES, None), P(("zl", "y", "core"), ("zh", "x"), None)),
        check_vma=False,
    )
```

```python
import functools

import jax
import jax.numpy as jnp
from jax import lax
from jax.experimental import pallas as pl
from jax.experimental.pallas import tpu as pltpu
from jax.sharding import Mesh
from jax.sharding import PartitionSpec as P

region_rate = 0.05
item_rate = 0.01
decay_rate = 0.1

AXES = ("zh", "x", "zl", "y", "core")
Z_RING = ("zh", "zl")


def grad_kernel(first, last, ny, rows_ref, counts_ref, sel_ref, u_ref, v_ref, slab0_ref, slab1_ref, *rest):
    if first:
        region_ref, item_ref = rest
    else:
        region_in_ref, region_ref, item_ref = rest
    step = pl.program_id(0)
    slots, block = slab0_ref.shape[1], slab0_ref.shape[2]
    pairs = ny // 2
    zl = step // pairs
    pair = step % pairs

    @pl.when(step == 0)
    def _():
        if first:
            region_ref[...] = jnp.zeros_like(region_ref)
        else:
            region_ref[...] = region_in_ref[...]

    for g, slab_ref in enumerate((slab0_ref, slab1_ref)):
        panel = (zl * ny + 2 * pair + g) * 2 + sel_ref[0]
        count = counts_ref[panel]
        v = v_ref[g, 0]
        half = slots // 2

        def slot_range(lo, hi, g=g, slab_ref=slab_ref, panel=panel, count=count, v=v):
            chosen_rows = [rows_ref[panel * slots + s] for s in range(lo, hi)]
            chosen = jnp.concatenate([u_ref[b] for b in chosen_rows], axis=0)
            predicted = lax.dot_general(
                chosen, v, (((1,), (1,)), ((), ())), preferred_element_type=jnp.float32
            )
            tiles = slab_ref[0, lo:hi].reshape((hi - lo) * block, block).astype(jnp.float32)
            slot_of = lo + lax.broadcasted_iota(jnp.int32, ((hi - lo) * block, block), 0) // block
            residual = jnp.where(slot_of < count, predicted - tiles, 0.0).astype(jnp.bfloat16)
            term = lax.dot_general(
                residual, chosen, (((0,), (0,)), ((), ())), preferred_element_type=jnp.float32
            )
            if lo == 0:
                item_ref[g, 0] = term
            else:
                item_ref[g, 0] += term
            terms = jnp.dot(residual, v, preferred_element_type=jnp.float32)
            for s, b in enumerate(chosen_rows):
                region_ref[b] += terms[s * block:(s + 1) * block]

        slot_range(0, half)
        pl.when(count > half)(lambda: slot_range(half, slots))

    if last:
        @pl.when(step == pl.num_programs(0) - 1)
        def _():
            wide = u_ref[...].astype(jnp.float32)
            region_ref[...] = wide - region_rate * (region_ref[...] + decay_rate * wide)


def local_grads(region_blocks, panels, tiles, rows_flat, counts, core_sel, region_in, last):
    row_blocks, block, width = region_blocks.shape
    ny, nzl = panels.shape[:2]
    slots = tiles.shape[1]
    pairs = ny // 2
    first = region_in is None

    def slab_map(g):
        return lambda i, r, c, s: (((i // pairs) * ny + 2 * (i % pairs) + g) * 2 + s[0], 0, 0, 0)

    in_specs = [
        pl.BlockSpec((row_blocks, block, width), lambda i, r, c, s: (0, 0, 0)),
        pl.BlockSpec((2, 1, block, width), lambda i, r, c, s: (i % pairs, i // pairs, 0, 0)),
        pl.BlockSpec((1, slots, block, block), slab_map(0)),
        pl.BlockSpec((1, slots, block, block), slab_map(1)),
    ]
    operands = [region_blocks, panels, tiles, tiles]
    aliases = {}
    if not first:
        in_specs.append(pl.BlockSpec((row_blocks, block, width), lambda i, r, c, s: (0, 0, 0)))
        operands.append(region_in)
        aliases = {3 + len(operands) - 1: 0}
    grid_spec = pltpu.PrefetchScalarGridSpec(
        num_scalar_prefetch=3,
        grid=(ny * nzl // 2,),
        in_specs=in_specs,
        out_specs=[
            pl.BlockSpec((row_blocks, block, width), lambda i, r, c, s: (0, 0, 0)),
            pl.BlockSpec((2, 1, block, width), lambda i, r, c, s: (i % pairs, i // pairs, 0, 0)),
        ],
    )
    n_panels = ny * nzl
    flops = 3 * 2 * n_panels * slots * block * block * width
    bytes_accessed = (
        region_blocks.size * 2 + panels.size * 2 + n_panels * slots * block * block * 2
        + region_blocks.size * 8 + panels.size * 4
    )
    return pl.pallas_call(
        functools.partial(grad_kernel, first, last, ny),
        grid_spec=grid_spec,
        out_shape=[
            jax.ShapeDtypeStruct((row_blocks, block, width), jnp.float32),
            jax.ShapeDtypeStruct((ny, nzl, block, width), jnp.float32),
        ],
        input_output_aliases=aliases,
        compiler_params=pltpu.CompilerParams(
            dimension_semantics=("arbitrary",),
            vmem_limit_bytes=48 * 1024 * 1024,
        ),
        cost_estimate=pl.CostEstimate(
            flops=flops, bytes_accessed=bytes_accessed, transcendentals=0
        ),
    )(rows_flat, counts, core_sel, *operands)


def take(arr, index):
    return lax.dynamic_index_in_dim(arr, index, 0, keepdims=False)


def put(arr, value, index):
    return lax.dynamic_update_index_in_dim(arr, value, index, 0)


def ring_pairs(n, step):
    return [(s, (s + step) % n) for s in range(n)]


def rings_reduce_scatter(jobs):
    state = []
    for x, axes, n in jobs:
        me = lax.axis_index(axes)
        half = x.shape[1] // 2
        ahead, behind = x[:, :half], x[:, half:]
        state.append([ahead, behind, axes, n, me, take(ahead, (me - 1) % n), take(behind, (me + 1) % n)])
    for t in range(max(job[2] for job in jobs) - 1):
        for st in state:
            ahead, behind, axes, n, me, acc_a, acc_b = st
            if t >= n - 1:
                continue
            got_a = lax.ppermute(acc_a, axes, ring_pairs(n, 1))
            got_b = lax.ppermute(acc_b, axes, ring_pairs(n, n - 1))
            st[5] = got_a + take(ahead, (me - 2 - t) % n)
            st[6] = got_b + take(behind, (me + 2 + t) % n)
    return [jnp.concatenate([st[5], st[6]], axis=0) for st in state]


def rings_all_gather(jobs):
    state = []
    for x, axes, n in jobs:
        me = lax.axis_index(axes)
        half = x.shape[0] // 2
        cur_a, cur_b = x[:half], x[half:]
        buf_a = put(jnp.zeros((n,) + cur_a.shape, x.dtype), cur_a, me)
        buf_b = put(jnp.zeros((n,) + cur_b.shape, x.dtype), cur_b, me)
        state.append([axes, n, me, cur_a, cur_b, buf_a, buf_b])
    for t in range(max(job[2] for job in jobs) - 1):
        for st in state:
            axes, n, me, cur_a, cur_b, buf_a, buf_b = st
            if t >= n - 1:
                continue
            cur_a = lax.ppermute(cur_a, axes, ring_pairs(n, 1))
            cur_b = lax.ppermute(cur_b, axes, ring_pairs(n, n - 1))
            st[3], st[4] = cur_a, cur_b
            st[5] = put(buf_a, cur_a, (me - 1 - t) % n)
            st[6] = put(buf_b, cur_b, (me + 1 + t) % n)
    return [jnp.concatenate([st[5], st[6]], axis=1) for st in state]


def direct_reduce_scatter(jobs):
    outs = []
    for x, axes, n in jobs:
        me = lax.axis_index(axes)
        total = take(x, me)
        for k in range(1, n):
            total = total + lax.ppermute(take(x, (me + k) % n), axes, ring_pairs(n, k))
        outs.append(total)
    return outs


def direct_all_gather(jobs):
    outs = []
    for x, axes, n in jobs:
        me = lax.axis_index(axes)
        buf = put(jnp.zeros((n,) + x.shape, x.dtype), x, me)
        for k in range(1, n):
            buf = put(buf, lax.ppermute(x, axes, ring_pairs(n, k)), (me - k) % n)
        outs.append(buf)
    return outs


def on_device(region_factors, item_factors, slab_blocks, block_rows, counts):
    n_zh, n_x = lax.axis_size("zh"), lax.axis_size("x")
    n_zl, n_y, n_core = lax.axis_size("zl"), lax.axis_size("y"), lax.axis_size("core")
    block = slab_blocks.shape[-1]
    width = region_factors.shape[-1]
    jj = block // (n_zh * n_x)
    hw = width // 2
    row_blocks = region_factors.shape[0] // block
    region_blocks = region_factors.reshape(row_blocks, block, width)

    piece = item_factors[0]
    (got,) = direct_all_gather([(piece, "zh", n_zh)])
    (got,) = direct_all_gather([(got, "zl", n_zl)])
    part_a, part_b = direct_all_gather([(got[..., :hw], "x", n_x), (got[..., hw:], "y", n_y)])
    part_a, part_b = direct_all_gather([(part_a, "y", n_y), (part_b, "x", n_x)])
    part_a = part_a.transpose(0, 2, 3, 1, 4, 5)
    part_b = part_b.transpose(1, 2, 3, 0, 4, 5)
    panel_y = jnp.concatenate([part_a, part_b], axis=-1).reshape(n_y, n_zl, block, width)
    swap = ring_pairs(n_core, 1)
    panel_other = lax.ppermute(panel_y, "core", swap)

    me = lax.axis_index("core")
    tiles, rows_flat, live = slab_blocks[0], block_rows[0].reshape(-1), counts[0]
    partial_regions, other_part = local_grads(
        region_blocks, panel_other, tiles, rows_flat, live, (1 - me)[None], None, False
    )
    got = lax.ppermute(other_part, "core", swap)
    new_regions, own_part = local_grads(
        region_blocks, panel_y, tiles, rows_flat, live, me[None], partial_regions, True
    )

    grad = own_part + got
    grad = grad.reshape(n_y, n_zl, n_zh, n_x, jj, width)
    part_a = grad[..., :hw]
    part_b = grad[..., hw:].transpose(3, 0, 1, 2, 4, 5)
    part_a, part_b = rings_reduce_scatter([(part_a, "y", n_y), (part_b, "x", n_x)])
    part_a = part_a.transpose(2, 0, 1, 3, 4)
    part_a, part_b = direct_reduce_scatter([(part_a, "x", n_x), (part_b, "y", n_y)])
    grad = jnp.concatenate([part_a, part_b], axis=-1)
    (grad,) = direct_reduce_scatter([(grad, "zl", n_zl)])
    (own_grad,) = direct_reduce_scatter([(grad, "zh", n_zh)])

    own_rows = piece.astype(jnp.float32)
    new_items = own_rows - item_rate * (own_grad + decay_rate * own_rows)
    return (new_regions.reshape(row_blocks * block, width), new_items[None])


def solution(mesh):
    rows, cols = mesh.devices.shape
    n_zh = 2
    n_core = 2
    n_x = rows // n_zh
    n_y = 4
    n_zl = cols // (n_y * n_core)
    fine = Mesh(mesh.devices.reshape(n_zh, n_x, n_zl, n_y, n_core), AXES)
    return jax.shard_map(
        on_device,
        mesh=fine,
        in_specs=(
            P(AXES, None),
            P(("zl", "y", "core"), ("zh", "x"), None),
            P(AXES, None, None, None, None),
            P(AXES, None, None),
            P(AXES, None),
        ),
        out_specs=(P(AXES, None), P(("zl", "y", "core"), ("zh", "x"), None)),
        check_vma=False,
    )
```

```python
import functools

import jax
import jax.numpy as jnp
from jax import lax
from jax.experimental import pallas as pl
from jax.experimental.pallas import tpu as pltpu
from jax.sharding import Mesh
from jax.sharding import PartitionSpec as P

region_rate = 0.05
item_rate = 0.01
decay_rate = 0.1

AXES = ("zh", "x", "zl", "y", "core")
Z_RING = ("zh", "zl")


def grad_kernel(first, last, ny, rows_ref, counts_ref, sel_ref, u_ref, v_ref, slab0_ref, slab1_ref, *rest):
    if first:
        region_ref, item_ref = rest
    else:
        region_in_ref, region_ref, item_ref = rest
    step = pl.program_id(0)
    slots, block = slab0_ref.shape[1], slab0_ref.shape[2]
    pairs = ny // 2
    zl = step // pairs
    pair = step % pairs

    @pl.when(step == 0)
    def _():
        if first:
            region_ref[...] = jnp.zeros_like(region_ref)
        else:
            region_ref[...] = region_in_ref[...]

    for g, slab_ref in enumerate((slab0_ref, slab1_ref)):
        panel = (zl * ny + 2 * pair + g) * 2 + sel_ref[0]
        count = counts_ref[panel]
        v = v_ref[g, 0]
        chosen_rows = [rows_ref[panel * slots + s] for s in range(slots)]
        chosen = jnp.concatenate([u_ref[b] for b in chosen_rows], axis=0)
        predicted = lax.dot_general(
            chosen, v, (((1,), (1,)), ((), ())), preferred_element_type=jnp.float32
        )
        tiles = slab_ref[0].reshape(slots * block, block).astype(jnp.float32)
        slot_of = lax.broadcasted_iota(jnp.int32, (slots * block, block), 0) // block
        residual = jnp.where(slot_of < count, predicted - tiles, 0.0).astype(jnp.bfloat16)
        item_ref[g, 0] = lax.dot_general(
            residual, chosen, (((0,), (0,)), ((), ())), preferred_element_type=jnp.float32
        )
        terms = jnp.dot(residual, v, preferred_element_type=jnp.float32)
        for s, b in enumerate(chosen_rows):
            region_ref[b] += terms[s * block:(s + 1) * block]

    if last:
        @pl.when(step == pl.num_programs(0) - 1)
        def _():
            wide = u_ref[...].astype(jnp.float32)
            region_ref[...] = wide - region_rate * (region_ref[...] + decay_rate * wide)


def local_grads(region_blocks, panels, tiles, rows_flat, counts, core_sel, region_in, last):
    row_blocks, block, width = region_blocks.shape
    ny, nzl = panels.shape[:2]
    slots = tiles.shape[1]
    pairs = ny // 2
    first = region_in is None

    def slab_map(g):
        return lambda i, r, c, s: (((i // pairs) * ny + 2 * (i % pairs) + g) * 2 + s[0], 0, 0, 0)

    in_specs = [
        pl.BlockSpec((row_blocks, block, width), lambda i, r, c, s: (0, 0, 0)),
        pl.BlockSpec((2, 1, block, width), lambda i, r, c, s: (i % pairs, i // pairs, 0, 0)),
        pl.BlockSpec((1, slots, block, block), slab_map(0)),
        pl.BlockSpec((1, slots, block, block), slab_map(1)),
    ]
    operands = [region_blocks, panels, tiles, tiles]
    aliases = {}
    if not first:
        in_specs.append(pl.BlockSpec((row_blocks, block, width), lambda i, r, c, s: (0, 0, 0)))
        operands.append(region_in)
        aliases = {3 + len(operands) - 1: 0}
    grid_spec = pltpu.PrefetchScalarGridSpec(
        num_scalar_prefetch=3,
        grid=(ny * nzl // 2,),
        in_specs=in_specs,
        out_specs=[
            pl.BlockSpec((row_blocks, block, width), lambda i, r, c, s: (0, 0, 0)),
            pl.BlockSpec((2, 1, block, width), lambda i, r, c, s: (i % pairs, i // pairs, 0, 0)),
        ],
    )
    n_panels = ny * nzl
    flops = 3 * 2 * n_panels * slots * block * block * width
    bytes_accessed = (
        region_blocks.size * 2 + panels.size * 2 + n_panels * slots * block * block * 2
        + region_blocks.size * 8 + panels.size * 4
    )
    return pl.pallas_call(
        functools.partial(grad_kernel, first, last, ny),
        grid_spec=grid_spec,
        out_shape=[
            jax.ShapeDtypeStruct((row_blocks, block, width), jnp.float32),
            jax.ShapeDtypeStruct((ny, nzl, block, width), jnp.float32),
        ],
        input_output_aliases=aliases,
        compiler_params=pltpu.CompilerParams(
            dimension_semantics=("arbitrary",),
            vmem_limit_bytes=48 * 1024 * 1024,
        ),
        cost_estimate=pl.CostEstimate(
            flops=flops, bytes_accessed=bytes_accessed, transcendentals=0
        ),
    )(rows_flat, counts, core_sel, *operands)


def take(arr, index):
    return lax.dynamic_index_in_dim(arr, index, 0, keepdims=False)


def put(arr, value, index):
    return lax.dynamic_update_index_in_dim(arr, value, index, 0)


def ring_pairs(n, step):
    return [(s, (s + step) % n) for s in range(n)]


def rings_reduce_scatter(jobs):
    state = []
    for x, axes, n in jobs:
        me = lax.axis_index(axes)
        half = x.shape[1] // 2
        ahead, behind = x[:, :half], x[:, half:]
        state.append([ahead, behind, axes, n, me, take(ahead, (me - 1) % n), take(behind, (me + 1) % n)])
    for t in range(max(job[2] for job in jobs) - 1):
        for st in state:
            ahead, behind, axes, n, me, acc_a, acc_b = st
            if t >= n - 1:
                continue
            got_a = lax.ppermute(acc_a, axes, ring_pairs(n, 1))
            got_b = lax.ppermute(acc_b, axes, ring_pairs(n, n - 1))
            st[5] = got_a + take(ahead, (me - 2 - t) % n)
            st[6] = got_b + take(behind, (me + 2 + t) % n)
    return [jnp.concatenate([st[5], st[6]], axis=0) for st in state]


def rings_all_gather(jobs):
    state = []
    for x, axes, n in jobs:
        me = lax.axis_index(axes)
        half = x.shape[0] // 2
        cur_a, cur_b = x[:half], x[half:]
        buf_a = put(jnp.zeros((n,) + cur_a.shape, x.dtype), cur_a, me)
        buf_b = put(jnp.zeros((n,) + cur_b.shape, x.dtype), cur_b, me)
        state.append([axes, n, me, cur_a, cur_b, buf_a, buf_b])
    for t in range(max(job[2] for job in jobs) - 1):
        for st in state:
            axes, n, me, cur_a, cur_b, buf_a, buf_b = st
            if t >= n - 1:
                continue
            cur_a = lax.ppermute(cur_a, axes, ring_pairs(n, 1))
            cur_b = lax.ppermute(cur_b, axes, ring_pairs(n, n - 1))
            st[3], st[4] = cur_a, cur_b
            st[5] = put(buf_a, cur_a, (me - 1 - t) % n)
            st[6] = put(buf_b, cur_b, (me + 1 + t) % n)
    return [jnp.concatenate([st[5], st[6]], axis=1) for st in state]


def direct_reduce_scatter(jobs):
    outs = []
    for x, axes, n in jobs:
        me = lax.axis_index(axes)
        total = take(x, me)
        for k in range(1, n):
            total = total + lax.ppermute(take(x, (me + k) % n), axes, ring_pairs(n, k))
        outs.append(total)
    return outs


def direct_all_gather(jobs):
    outs = []
    for x, axes, n in jobs:
        me = lax.axis_index(axes)
        buf = put(jnp.zeros((n,) + x.shape, x.dtype), x, me)
        for k in range(1, n):
            buf = put(buf, lax.ppermute(x, axes, ring_pairs(n, k)), (me - k) % n)
        outs.append(buf)
    return outs


def on_device(region_factors, item_factors, slab_blocks, block_rows, counts):
    n_zh, n_x = lax.axis_size("zh"), lax.axis_size("x")
    n_zl, n_y, n_core = lax.axis_size("zl"), lax.axis_size("y"), lax.axis_size("core")
    block = slab_blocks.shape[-1]
    width = region_factors.shape[-1]
    jj = block // (n_zh * n_x)
    hw = width // 2
    row_blocks = region_factors.shape[0] // block
    region_blocks = region_factors.reshape(row_blocks, block, width)

    piece = item_factors[0]
    (got,) = direct_all_gather([(piece, "zh", n_zh)])
    (got,) = direct_all_gather([(got, "zl", n_zl)])
    part_a, part_b = direct_all_gather([(got[..., :hw], "x", n_x), (got[..., hw:], "y", n_y)])
    part_a, part_b = direct_all_gather([(part_a, "y", n_y), (part_b, "x", n_x)])
    part_a = part_a.transpose(0, 2, 3, 1, 4, 5)
    part_b = part_b.transpose(1, 2, 3, 0, 4, 5)
    panel_y = jnp.concatenate([part_a, part_b], axis=-1).reshape(n_y, n_zl, block, width)
    swap = ring_pairs(n_core, 1)
    panel_other = lax.ppermute(panel_y, "core", swap)

    me = lax.axis_index("core")
    tiles, rows_flat, live = slab_blocks[0], block_rows[0].reshape(-1), counts[0]
    partial_regions, other_part = local_grads(
        region_blocks, panel_other, tiles, rows_flat, live, (1 - me)[None], None, False
    )
    got = lax.ppermute(other_part, "core", swap)
    new_regions, own_part = local_grads(
        region_blocks, panel_y, tiles, rows_flat, live, me[None], partial_regions, True
    )

    own_part = own_part.reshape(n_y, n_zl, n_zh, n_x, jj, width)
    got = got.reshape(n_y, n_zl, n_zh, n_x, jj, width)
    part_a = own_part[..., :hw] + got[..., :hw]
    part_b = (own_part[..., hw:] + got[..., hw:]).transpose(3, 0, 1, 2, 4, 5)
    part_a, part_b = rings_reduce_scatter([(part_a, "y", n_y), (part_b, "x", n_x)])
    part_a = part_a.transpose(2, 0, 1, 3, 4)
    part_a, part_b = direct_reduce_scatter([(part_a, "x", n_x), (part_b, "y", n_y)])
    grad = jnp.concatenate([part_a, part_b], axis=-1)
    (grad,) = direct_reduce_scatter([(grad, "zl", n_zl)])
    (own_grad,) = direct_reduce_scatter([(grad, "zh", n_zh)])

    own_rows = piece.astype(jnp.float32)
    new_items = own_rows - item_rate * (own_grad + decay_rate * own_rows)
    return (new_regions.reshape(row_blocks * block, width), new_items[None])


def solution(mesh):
    rows, cols = mesh.devices.shape
    n_zh = 2
    n_core = 2
    n_x = rows // n_zh
    n_y = 4
    n_zl = cols // (n_y * n_core)
    fine = Mesh(mesh.devices.reshape(n_zh, n_x, n_zl, n_y, n_core), AXES)
    return jax.shard_map(
        on_device,
        mesh=fine,
        in_specs=(
            P(AXES, None),
            P(("zl", "y", "core"), ("zh", "x"), None),
            P(AXES, None, None, None, None),
            P(AXES, None, None),
            P(AXES, None),
        ),
        out_specs=(P(AXES, None), P(("zl", "y", "core"), ("zh", "x"), None)),
        check_vma=False,
    )
```

```python
import functools

import jax
import jax.numpy as jnp
from jax import lax
from jax.experimental import pallas as pl
from jax.experimental.pallas import tpu as pltpu
from jax.sharding import Mesh
from jax.sharding import PartitionSpec as P

region_rate = 0.05
item_rate = 0.01
decay_rate = 0.1

AXES = ("zh", "x", "zl", "y", "core")
Z_RING = ("zh", "zl")


def grad_kernel(first, last, ny, zl0, rows_ref, counts_ref, sel_ref, u_ref, v_ref, slab0_ref, slab1_ref, *rest):
    if first:
        region_ref, item_ref = rest
    else:
        region_in_ref, region_ref, item_ref = rest
    step = pl.program_id(0)
    slots, block = slab0_ref.shape[1], slab0_ref.shape[2]
    pairs = ny // 2
    zl = zl0 + step // pairs
    pair = step % pairs

    @pl.when(step == 0)
    def _():
        if first:
            region_ref[...] = jnp.zeros_like(region_ref)
        else:
            region_ref[...] = region_in_ref[...]

    for g, slab_ref in enumerate((slab0_ref, slab1_ref)):
        panel = (zl * ny + 2 * pair + g) * 2 + sel_ref[0]
        count = counts_ref[panel]
        v = v_ref[g, 0]
        chosen_rows = [rows_ref[panel * slots + s] for s in range(slots)]
        chosen = jnp.concatenate([u_ref[b] for b in chosen_rows], axis=0)
        predicted = lax.dot_general(
            chosen, v, (((1,), (1,)), ((), ())), preferred_element_type=jnp.float32
        )
        tiles = slab_ref[0].reshape(slots * block, block).astype(jnp.float32)
        slot_of = lax.broadcasted_iota(jnp.int32, (slots * block, block), 0) // block
        residual = jnp.where(slot_of < count, predicted - tiles, 0.0).astype(jnp.bfloat16)
        item_ref[g, 0] = lax.dot_general(
            residual, chosen, (((0,), (0,)), ((), ())), preferred_element_type=jnp.float32
        )
        terms = jnp.dot(residual, v, preferred_element_type=jnp.float32)
        for s, b in enumerate(chosen_rows):
            region_ref[b] += terms[s * block:(s + 1) * block]

    if last:
        @pl.when(step == pl.num_programs(0) - 1)
        def _():
            wide = u_ref[...].astype(jnp.float32)
            region_ref[...] = wide - region_rate * (region_ref[...] + decay_rate * wide)


def local_grads(region_blocks, panels, tiles, rows_flat, counts, core_sel, region_in, last, zl0, nzl_sub):
    row_blocks, block, width = region_blocks.shape
    ny, nzl = panels.shape[:2]
    slots = tiles.shape[1]
    pairs = ny // 2
    first = region_in is None

    def slab_map(g):
        return lambda i, r, c, s: (((zl0 + i // pairs) * ny + 2 * (i % pairs) + g) * 2 + s[0], 0, 0, 0)

    in_specs = [
        pl.BlockSpec((row_blocks, block, width), lambda i, r, c, s: (0, 0, 0)),
        pl.BlockSpec((2, 1, block, width), lambda i, r, c, s: (i % pairs, zl0 + i // pairs, 0, 0)),
        pl.BlockSpec((1, slots, block, block), slab_map(0)),
        pl.BlockSpec((1, slots, block, block), slab_map(1)),
    ]
    operands = [region_blocks, panels, tiles, tiles]
    aliases = {}
    if not first:
        in_specs.append(pl.BlockSpec((row_blocks, block, width), lambda i, r, c, s: (0, 0, 0)))
        operands.append(region_in)
        aliases = {3 + len(operands) - 1: 0}
    grid_spec = pltpu.PrefetchScalarGridSpec(
        num_scalar_prefetch=3,
        grid=(ny * nzl_sub // 2,),
        in_specs=in_specs,
        out_specs=[
            pl.BlockSpec((row_blocks, block, width), lambda i, r, c, s: (0, 0, 0)),
            pl.BlockSpec((2, 1, block, width), lambda i, r, c, s: (i % pairs, i // pairs, 0, 0)),
        ],
    )
    n_panels = ny * nzl_sub
    flops = 3 * 2 * n_panels * slots * block * block * width
    bytes_accessed = (
        region_blocks.size * 2 + n_panels * block * width * 2 + n_panels * slots * block * block * 2
        + region_blocks.size * 8 + n_panels * block * width * 4
    )
    return pl.pallas_call(
        functools.partial(grad_kernel, first, last, ny, zl0),
        grid_spec=grid_spec,
        out_shape=[
            jax.ShapeDtypeStruct((row_blocks, block, width), jnp.float32),
            jax.ShapeDtypeStruct((ny, nzl_sub, block, width), jnp.float32),
        ],
        input_output_aliases=aliases,
        compiler_params=pltpu.CompilerParams(
            dimension_semantics=("arbitrary",),
            vmem_limit_bytes=48 * 1024 * 1024,
        ),
        cost_estimate=pl.CostEstimate(
            flops=flops, bytes_accessed=bytes_accessed, transcendentals=0
        ),
    )(rows_flat, counts, core_sel, *operands)


def take(arr, index):
    return lax.dynamic_index_in_dim(arr, index, 0, keepdims=False)


def put(arr, value, index):
    return lax.dynamic_update_index_in_dim(arr, value, index, 0)


def ring_pairs(n, step):
    return [(s, (s + step) % n) for s in range(n)]


def rings_reduce_scatter(jobs):
    state = []
    for x, axes, n in jobs:
        me = lax.axis_index(axes)
        half = x.shape[1] // 2
        ahead, behind = x[:, :half], x[:, half:]
        state.append([ahead, behind, axes, n, me, take(ahead, (me - 1) % n), take(behind, (me + 1) % n)])
    for t in range(max(job[2] for job in jobs) - 1):
        for st in state:
            ahead, behind, axes, n, me, acc_a, acc_b = st
            if t >= n - 1:
                continue
            got_a = lax.ppermute(acc_a, axes, ring_pairs(n, 1))
            got_b = lax.ppermute(acc_b, axes, ring_pairs(n, n - 1))
            st[5] = got_a + take(ahead, (me - 2 - t) % n)
            st[6] = got_b + take(behind, (me + 2 + t) % n)
    return [jnp.concatenate([st[5], st[6]], axis=0) for st in state]


def rings_all_gather(jobs):
    state = []
    for x, axes, n in jobs:
        me = lax.axis_index(axes)
        half = x.shape[0] // 2
        cur_a, cur_b = x[:half], x[half:]
        buf_a = put(jnp.zeros((n,) + cur_a.shape, x.dtype), cur_a, me)
        buf_b = put(jnp.zeros((n,) + cur_b.shape, x.dtype), cur_b, me)
        state.append([axes, n, me, cur_a, cur_b, buf_a, buf_b])
    for t in range(max(job[2] for job in jobs) - 1):
        for st in state:
            axes, n, me, cur_a, cur_b, buf_a, buf_b = st
            if t >= n - 1:
                continue
            cur_a = lax.ppermute(cur_a, axes, ring_pairs(n, 1))
            cur_b = lax.ppermute(cur_b, axes, ring_pairs(n, n - 1))
            st[3], st[4] = cur_a, cur_b
            st[5] = put(buf_a, cur_a, (me - 1 - t) % n)
            st[6] = put(buf_b, cur_b, (me + 1 + t) % n)
    return [jnp.concatenate([st[5], st[6]], axis=1) for st in state]


def direct_reduce_scatter(jobs):
    outs = []
    for x, axes, n in jobs:
        me = lax.axis_index(axes)
        total = take(x, me)
        for k in range(1, n):
            total = total + lax.ppermute(take(x, (me + k) % n), axes, ring_pairs(n, k))
        outs.append(total)
    return outs


def direct_all_gather(jobs):
    outs = []
    for x, axes, n in jobs:
        me = lax.axis_index(axes)
        buf = put(jnp.zeros((n,) + x.shape, x.dtype), x, me)
        for k in range(1, n):
            buf = put(buf, lax.ppermute(x, axes, ring_pairs(n, k)), (me - k) % n)
        outs.append(buf)
    return outs


def on_device(region_factors, item_factors, slab_blocks, block_rows, counts):
    n_zh, n_x = lax.axis_size("zh"), lax.axis_size("x")
    n_zl, n_y, n_core = lax.axis_size("zl"), lax.axis_size("y"), lax.axis_size("core")
    block = slab_blocks.shape[-1]
    width = region_factors.shape[-1]
    jj = block // (n_zh * n_x)
    hw = width // 2
    row_blocks = region_factors.shape[0] // block
    region_blocks = region_factors.reshape(row_blocks, block, width)

    piece = item_factors[0]
    (got,) = direct_all_gather([(piece, "zh", n_zh)])
    (got,) = direct_all_gather([(got, "zl", n_zl)])
    part_a, part_b = direct_all_gather([(got[..., :hw], "x", n_x), (got[..., hw:], "y", n_y)])
    part_a, part_b = direct_all_gather([(part_a, "y", n_y), (part_b, "x", n_x)])
    part_a = part_a.transpose(0, 2, 3, 1, 4, 5)
    part_b = part_b.transpose(1, 2, 3, 0, 4, 5)
    panel_y = jnp.concatenate([part_a, part_b], axis=-1).reshape(n_y, n_zl, block, width)
    swap = ring_pairs(n_core, 1)
    panel_other = lax.ppermute(panel_y, "core", swap)

    me = lax.axis_index("core")
    tiles, rows_flat, live = slab_blocks[0], block_rows[0].reshape(-1), counts[0]
    lo = n_zl // 2
    early_regions, own_early = local_grads(
        region_blocks, panel_y, tiles, rows_flat, live, me[None], None, False, 0, lo
    )
    partial_regions, other_part = local_grads(
        region_blocks, panel_other, tiles, rows_flat, live, (1 - me)[None], early_regions, False, 0, n_zl
    )
    got = lax.ppermute(other_part, "core", swap)
    new_regions, own_late = local_grads(
        region_blocks, panel_y, tiles, rows_flat, live, me[None], partial_regions, True, lo, n_zl - lo
    )
    own_part = jnp.concatenate([own_early, own_late], axis=1)

    own_part = own_part.reshape(n_y, n_zl, n_zh, n_x, jj, width)
    got = got.reshape(n_y, n_zl, n_zh, n_x, jj, width)
    part_a = own_part[..., :hw] + got[..., :hw]
    part_b = (own_part[..., hw:] + got[..., hw:]).transpose(3, 0, 1, 2, 4, 5)
    part_a, part_b = rings_reduce_scatter([(part_a, "y", n_y), (part_b, "x", n_x)])
    part_a = part_a.transpose(2, 0, 1, 3, 4)
    part_a, part_b = direct_reduce_scatter([(part_a, "x", n_x), (part_b, "y", n_y)])
    grad = jnp.concatenate([part_a, part_b], axis=-1)
    (grad,) = direct_reduce_scatter([(grad, "zl", n_zl)])
    (own_grad,) = direct_reduce_scatter([(grad, "zh", n_zh)])

    own_rows = piece.astype(jnp.float32)
    new_items = own_rows - item_rate * (own_grad + decay_rate * own_rows)
    return (new_regions.reshape(row_blocks * block, width), new_items[None])


def solution(mesh):
    rows, cols = mesh.devices.shape
    n_zh = 2
    n_core = 2
    n_x = rows // n_zh
    n_y = 4
    n_zl = cols // (n_y * n_core)
    fine = Mesh(mesh.devices.reshape(n_zh, n_x, n_zl, n_y, n_core), AXES)
    return jax.shard_map(
        on_device,
        mesh=fine,
        in_specs=(
            P(AXES, None),
            P(("zl", "y", "core"), ("zh", "x"), None),
            P(AXES, None, None, None, None),
            P(AXES, None, None),
            P(AXES, None),
        ),
        out_specs=(P(AXES, None), P(("zl", "y", "core"), ("zh", "x"), None)),
        check_vma=False,
    )
```

```python
import functools

import jax
import jax.numpy as jnp
from jax import lax
from jax.experimental import pallas as pl
from jax.experimental.pallas import tpu as pltpu
from jax.sharding import Mesh
from jax.sharding import PartitionSpec as P

region_rate = 0.05
item_rate = 0.01
decay_rate = 0.1

AXES = ("zh", "x", "zl", "y", "core")
Z_RING = ("zh", "zl")


def grad_kernel(first, last, ny, rows_ref, counts_ref, sel_ref, u_ref, v_ref, slab0_ref, slab1_ref, *rest):
    if first:
        region_ref, item_ref = rest
    else:
        region_in_ref, region_ref, item_ref = rest
    step = pl.program_id(0)
    slots, block = slab0_ref.shape[1], slab0_ref.shape[2]
    pairs = ny // 2
    zl = step // pairs
    pair = step % pairs

    @pl.when(step == 0)
    def _():
        if first:
            region_ref[...] = jnp.zeros_like(region_ref)
        else:
            region_ref[...] = region_in_ref[...]

    for g, slab_ref in enumerate((slab0_ref, slab1_ref)):
        panel = (zl * ny + 2 * pair + g) * 2 + sel_ref[0]
        count = counts_ref[panel]
        v = v_ref[g, 0]
        half = slots // 2

        def slot_range(lo, hi, g=g, slab_ref=slab_ref, panel=panel, count=count, v=v):
            chosen_rows = [rows_ref[panel * slots + s] for s in range(lo, hi)]
            chosen = jnp.concatenate([u_ref[b] for b in chosen_rows], axis=0)
            predicted = lax.dot_general(
                chosen, v, (((1,), (1,)), ((), ())), preferred_element_type=jnp.float32
            )
            tiles = slab_ref[0, lo:hi].reshape((hi - lo) * block, block).astype(jnp.float32)
            slot_of = lo + lax.broadcasted_iota(jnp.int32, ((hi - lo) * block, block), 0) // block
            residual = jnp.where(slot_of < count, predicted - tiles, 0.0).astype(jnp.bfloat16)
            term = lax.dot_general(
                residual, chosen, (((0,), (0,)), ((), ())), preferred_element_type=jnp.float32
            )
            if lo == 0:
                item_ref[g, 0] = term
            else:
                item_ref[g, 0] += term
            terms = jnp.dot(residual, v, preferred_element_type=jnp.float32)
            for s, b in enumerate(chosen_rows):
                region_ref[b] += terms[s * block:(s + 1) * block]

        slot_range(0, half)
        pl.when(count > half)(lambda: slot_range(half, slots))

    if last:
        @pl.when(step == pl.num_programs(0) - 1)
        def _():
            wide = u_ref[...].astype(jnp.float32)
            region_ref[...] = wide - region_rate * (region_ref[...] + decay_rate * wide)


def local_grads(region_blocks, panels, tiles, rows_flat, counts, core_sel, region_in, last):
    row_blocks, block, width = region_blocks.shape
    ny, nzl = panels.shape[:2]
    slots = tiles.shape[1]
    pairs = ny // 2
    first = region_in is None

    def slab_map(g):
        return lambda i, r, c, s: (((i // pairs) * ny + 2 * (i % pairs) + g) * 2 + s[0], 0, 0, 0)

    in_specs = [
        pl.BlockSpec((row_blocks, block, width), lambda i, r, c, s: (0, 0, 0)),
        pl.BlockSpec((2, 1, block, width), lambda i, r, c, s: (i % pairs, i // pairs, 0, 0)),
        pl.BlockSpec((1, slots, block, block), slab_map(0)),
        pl.BlockSpec((1, slots, block, block), slab_map(1)),
    ]
    operands = [region_blocks, panels, tiles, tiles]
    aliases = {}
    if not first:
        in_specs.append(pl.BlockSpec((row_blocks, block, width), lambda i, r, c, s: (0, 0, 0)))
        operands.append(region_in)
        aliases = {3 + len(operands) - 1: 0}
    grid_spec = pltpu.PrefetchScalarGridSpec(
        num_scalar_prefetch=3,
        grid=(ny * nzl // 2,),
        in_specs=in_specs,
        out_specs=[
            pl.BlockSpec((row_blocks, block, width), lambda i, r, c, s: (0, 0, 0)),
            pl.BlockSpec((2, 1, block, width), lambda i, r, c, s: (i % pairs, i // pairs, 0, 0)),
        ],
    )
    n_panels = ny * nzl
    flops = 3 * 2 * n_panels * slots * block * block * width
    bytes_accessed = (
        region_blocks.size * 2 + panels.size * 2 + n_panels * slots * block * block * 2
        + region_blocks.size * 8 + panels.size * 4
    )
    return pl.pallas_call(
        functools.partial(grad_kernel, first, last, ny),
        grid_spec=grid_spec,
        out_shape=[
            jax.ShapeDtypeStruct((row_blocks, block, width), jnp.float32),
            jax.ShapeDtypeStruct((ny, nzl, block, width), jnp.float32),
        ],
        input_output_aliases=aliases,
        compiler_params=pltpu.CompilerParams(
            dimension_semantics=("arbitrary",),
            vmem_limit_bytes=48 * 1024 * 1024,
        ),
        cost_estimate=pl.CostEstimate(
            flops=flops, bytes_accessed=bytes_accessed, transcendentals=0
        ),
    )(rows_flat, counts, core_sel, *operands)


def take(arr, index):
    return lax.dynamic_index_in_dim(arr, index, 0, keepdims=False)


def put(arr, value, index):
    return lax.dynamic_update_index_in_dim(arr, value, index, 0)


def ring_pairs(n, step):
    return [(s, (s + step) % n) for s in range(n)]


def rings_reduce_scatter(jobs):
    state = []
    for x, axes, n in jobs:
        me = lax.axis_index(axes)
        half = x.shape[1] // 2
        ahead, behind = x[:, :half], x[:, half:]
        state.append([ahead, behind, axes, n, me, take(ahead, (me - 1) % n), take(behind, (me + 1) % n)])
    for t in range(max(job[2] for job in jobs) - 1):
        for st in state:
            ahead, behind, axes, n, me, acc_a, acc_b = st
            if t >= n - 1:
                continue
            got_a = lax.ppermute(acc_a, axes, ring_pairs(n, 1))
            got_b = lax.ppermute(acc_b, axes, ring_pairs(n, n - 1))
            st[5] = got_a + take(ahead, (me - 2 - t) % n)
            st[6] = got_b + take(behind, (me + 2 + t) % n)
    return [jnp.concatenate([st[5], st[6]], axis=0) for st in state]


def rings_all_gather(jobs):
    state = []
    for x, axes, n in jobs:
        me = lax.axis_index(axes)
        half = x.shape[0] // 2
        cur_a, cur_b = x[:half], x[half:]
        buf_a = put(jnp.zeros((n,) + cur_a.shape, x.dtype), cur_a, me)
        buf_b = put(jnp.zeros((n,) + cur_b.shape, x.dtype), cur_b, me)
        state.append([axes, n, me, cur_a, cur_b, buf_a, buf_b])
    for t in range(max(job[2] for job in jobs) - 1):
        for st in state:
            axes, n, me, cur_a, cur_b, buf_a, buf_b = st
            if t >= n - 1:
                continue
            cur_a = lax.ppermute(cur_a, axes, ring_pairs(n, 1))
            cur_b = lax.ppermute(cur_b, axes, ring_pairs(n, n - 1))
            st[3], st[4] = cur_a, cur_b
            st[5] = put(buf_a, cur_a, (me - 1 - t) % n)
            st[6] = put(buf_b, cur_b, (me + 1 + t) % n)
    return [jnp.concatenate([st[5], st[6]], axis=1) for st in state]


def direct_reduce_scatter(jobs):
    outs = []
    for x, axes, n in jobs:
        me = lax.axis_index(axes)
        total = take(x, me)
        for k in range(1, n):
            total = total + lax.ppermute(take(x, (me + k) % n), axes, ring_pairs(n, k))
        outs.append(total)
    return outs


def direct_all_gather(jobs):
    outs = []
    for x, axes, n in jobs:
        me = lax.axis_index(axes)
        buf = put(jnp.zeros((n,) + x.shape, x.dtype), x, me)
        for k in range(1, n):
            buf = put(buf, lax.ppermute(x, axes, ring_pairs(n, k)), (me - k) % n)
        outs.append(buf)
    return outs


def on_device(region_factors, item_factors, slab_blocks, block_rows, counts):
    n_zh, n_x = lax.axis_size("zh"), lax.axis_size("x")
    n_zl, n_y, n_core = lax.axis_size("zl"), lax.axis_size("y"), lax.axis_size("core")
    block = slab_blocks.shape[-1]
    width = region_factors.shape[-1]
    jj = block // (n_zh * n_x)
    hw = width // 2
    row_blocks = region_factors.shape[0] // block
    region_blocks = region_factors.reshape(row_blocks, block, width)

    piece = item_factors[0]
    (got,) = direct_all_gather([(piece, "zh", n_zh)])
    (got,) = direct_all_gather([(got, "zl", n_zl)])
    part_a, part_b = direct_all_gather([(got[..., :hw], "x", n_x), (got[..., hw:], "y", n_y)])
    part_a, part_b = direct_all_gather([(part_a, "y", n_y), (part_b, "x", n_x)])
    part_a = part_a.transpose(0, 2, 3, 1, 4, 5)
    part_b = part_b.transpose(1, 2, 3, 0, 4, 5)
    panel_y = jnp.concatenate([part_a, part_b], axis=-1).reshape(n_y, n_zl, block, width)
    swap = ring_pairs(n_core, 1)
    panel_other = lax.ppermute(panel_y, "core", swap)

    me = lax.axis_index("core")
    tiles, rows_flat, live = slab_blocks[0], block_rows[0].reshape(-1), counts[0]
    partial_regions, other_part = local_grads(
        region_blocks, panel_other, tiles, rows_flat, live, (1 - me)[None], None, False
    )
    got = lax.ppermute(other_part, "core", swap)
    new_regions, own_part = local_grads(
        region_blocks, panel_y, tiles, rows_flat, live, me[None], partial_regions, True
    )

    own_part = own_part.reshape(n_y, n_zl, n_zh, n_x, jj, width)
    got = got.reshape(n_y, n_zl, n_zh, n_x, jj, width)
    part_a = own_part[..., :hw] + got[..., :hw]
    part_b = (own_part[..., hw:] + got[..., hw:]).transpose(3, 0, 1, 2, 4, 5)
    part_a, part_b = rings_reduce_scatter([(part_a, "y", n_y), (part_b, "x", n_x)])
    part_a = part_a.transpose(2, 0, 1, 3, 4)
    part_a, part_b = direct_reduce_scatter([(part_a, "x", n_x), (part_b, "y", n_y)])
    grad = jnp.concatenate([part_a, part_b], axis=-1)
    (grad,) = direct_reduce_scatter([(grad, "zl", n_zl)])
    (own_grad,) = direct_reduce_scatter([(grad, "zh", n_zh)])

    own_rows = piece.astype(jnp.float32)
    new_items = own_rows - item_rate * (own_grad + decay_rate * own_rows)
    return (new_regions.reshape(row_blocks * block, width), new_items[None])


def solution(mesh):
    rows, cols = mesh.devices.shape
    n_zh = 2
    n_core = 2
    n_x = rows // n_zh
    n_y = 4
    n_zl = cols // (n_y * n_core)
    fine = Mesh(mesh.devices.reshape(n_zh, n_x, n_zl, n_y, n_core), AXES)
    return jax.shard_map(
        on_device,
        mesh=fine,
        in_specs=(
            P(AXES, None),
            P(("zl", "y", "core"), ("zh", "x"), None),
            P(AXES, None, None, None, None),
            P(AXES, None, None),
            P(AXES, None),
        ),
        out_specs=(P(AXES, None), P(("zl", "y", "core"), ("zh", "x"), None)),
        check_vma=False,
    )
```

```python
import functools

import jax
import jax.numpy as jnp
from jax import lax
from jax.experimental import pallas as pl
from jax.experimental.pallas import tpu as pltpu
from jax.sharding import Mesh
from jax.sharding import PartitionSpec as P

region_rate = 0.05
item_rate = 0.01
decay_rate = 0.1

AXES = ("zh", "x", "zl", "y", "core")
Z_RING = ("zh", "zl")


def grad_kernel(first, last, ny, rows_ref, counts_ref, sel_ref, u_ref, v_ref, slab0_ref, slab1_ref, *rest):
    if first:
        region_ref, item_ref = rest
    else:
        region_in_ref, region_ref, item_ref = rest
    step = pl.program_id(0)
    slots, block = slab0_ref.shape[1], slab0_ref.shape[2]
    pairs = ny // 2
    zl = step // pairs
    pair = step % pairs

    @pl.when(step == 0)
    def _():
        if first:
            region_ref[...] = jnp.zeros_like(region_ref)
        else:
            region_ref[...] = region_in_ref[...]

    for g, slab_ref in enumerate((slab0_ref, slab1_ref)):
        panel = (zl * ny + 2 * pair + g) * 2 + sel_ref[0]
        count = counts_ref[panel]
        v = v_ref[g, 0]
        chosen_rows = [rows_ref[panel * slots + s] for s in range(slots)]
        chosen = jnp.concatenate([u_ref[b] for b in chosen_rows], axis=0)
        predicted = lax.dot_general(
            chosen, v, (((1,), (1,)), ((), ())), preferred_element_type=jnp.float32
        )
        tiles = slab_ref[0].reshape(slots * block, block).astype(jnp.float32)
        slot_of = lax.broadcasted_iota(jnp.int32, (slots * block, block), 0) // block
        residual = jnp.where(slot_of < count, predicted - tiles, 0.0).astype(jnp.bfloat16)
        item_ref[g, 0] = lax.dot_general(
            residual, chosen, (((0,), (0,)), ((), ())), preferred_element_type=jnp.float32
        )
        terms = jnp.dot(residual, v, preferred_element_type=jnp.float32)
        for s, b in enumerate(chosen_rows):
            region_ref[b] += terms[s * block:(s + 1) * block]

    if last:
        @pl.when(step == pl.num_programs(0) - 1)
        def _():
            wide = u_ref[...].astype(jnp.float32)
            region_ref[...] = wide - region_rate * (region_ref[...] + decay_rate * wide)


def local_grads(region_blocks, panels, tiles, rows_flat, counts, core_sel, region_in, last):
    row_blocks, block, width = region_blocks.shape
    ny, nzl = panels.shape[:2]
    slots = tiles.shape[1]
    pairs = ny // 2
    first = region_in is None

    def slab_map(g):
        return lambda i, r, c, s: (((i // pairs) * ny + 2 * (i % pairs) + g) * 2 + s[0], 0, 0, 0)

    in_specs = [
        pl.BlockSpec((row_blocks, block, width), lambda i, r, c, s: (0, 0, 0)),
        pl.BlockSpec((2, 1, block, width), lambda i, r, c, s: (i % pairs, i // pairs, 0, 0)),
        pl.BlockSpec((1, slots, block, block), slab_map(0)),
        pl.BlockSpec((1, slots, block, block), slab_map(1)),
    ]
    operands = [region_blocks, panels, tiles, tiles]
    aliases = {}
    if not first:
        in_specs.append(pl.BlockSpec((row_blocks, block, width), lambda i, r, c, s: (0, 0, 0)))
        operands.append(region_in)
        aliases = {3 + len(operands) - 1: 0}
    grid_spec = pltpu.PrefetchScalarGridSpec(
        num_scalar_prefetch=3,
        grid=(ny * nzl // 2,),
        in_specs=in_specs,
        out_specs=[
            pl.BlockSpec((row_blocks, block, width), lambda i, r, c, s: (0, 0, 0)),
            pl.BlockSpec((2, 1, block, width), lambda i, r, c, s: (i % pairs, i // pairs, 0, 0)),
        ],
    )
    n_panels = ny * nzl
    flops = 3 * 2 * n_panels * slots * block * block * width
    bytes_accessed = (
        region_blocks.size * 2 + panels.size * 2 + n_panels * slots * block * block * 2
        + region_blocks.size * 8 + panels.size * 4
    )
    return pl.pallas_call(
        functools.partial(grad_kernel, first, last, ny),
        grid_spec=grid_spec,
        out_shape=[
            jax.ShapeDtypeStruct((row_blocks, block, width), jnp.float32),
            jax.ShapeDtypeStruct((ny, nzl, block, width), jnp.float32),
        ],
        input_output_aliases=aliases,
        compiler_params=pltpu.CompilerParams(
            dimension_semantics=("arbitrary",),
            vmem_limit_bytes=48 * 1024 * 1024,
        ),
        cost_estimate=pl.CostEstimate(
            flops=flops, bytes_accessed=bytes_accessed, transcendentals=0
        ),
    )(rows_flat, counts, core_sel, *operands)


def take(arr, index):
    return lax.dynamic_index_in_dim(arr, index, 0, keepdims=False)


def put(arr, value, index):
    return lax.dynamic_update_index_in_dim(arr, value, index, 0)


def ring_pairs(n, step):
    return [(s, (s + step) % n) for s in range(n)]


def rings_reduce_scatter(jobs):
    state = []
    for x, axes, n in jobs:
        me = lax.axis_index(axes)
        half = x.shape[1] // 2
        ahead, behind = x[:, :half], x[:, half:]
        state.append([ahead, behind, axes, n, me, take(ahead, (me - 1) % n), take(behind, (me + 1) % n)])
    for t in range(max(job[2] for job in jobs) - 1):
        for st in state:
            ahead, behind, axes, n, me, acc_a, acc_b = st
            if t >= n - 1:
                continue
            got_a = lax.ppermute(acc_a, axes, ring_pairs(n, 1))
            got_b = lax.ppermute(acc_b, axes, ring_pairs(n, n - 1))
            st[5] = got_a + take(ahead, (me - 2 - t) % n)
            st[6] = got_b + take(behind, (me + 2 + t) % n)
    return [jnp.concatenate([st[5], st[6]], axis=0) for st in state]


def rings_all_gather(jobs):
    state = []
    for x, axes, n in jobs:
        me = lax.axis_index(axes)
        half = x.shape[0] // 2
        cur_a, cur_b = x[:half], x[half:]
        buf_a = put(jnp.zeros((n,) + cur_a.shape, x.dtype), cur_a, me)
        buf_b = put(jnp.zeros((n,) + cur_b.shape, x.dtype), cur_b, me)
        state.append([axes, n, me, cur_a, cur_b, buf_a, buf_b])
    for t in range(max(job[2] for job in jobs) - 1):
        for st in state:
            axes, n, me, cur_a, cur_b, buf_a, buf_b = st
            if t >= n - 1:
                continue
            cur_a = lax.ppermute(cur_a, axes, ring_pairs(n, 1))
            cur_b = lax.ppermute(cur_b, axes, ring_pairs(n, n - 1))
            st[3], st[4] = cur_a, cur_b
            st[5] = put(buf_a, cur_a, (me - 1 - t) % n)
            st[6] = put(buf_b, cur_b, (me + 1 + t) % n)
    return [jnp.concatenate([st[5], st[6]], axis=1) for st in state]


def direct_reduce_scatter(jobs):
    outs = []
    for x, axes, n in jobs:
        me = lax.axis_index(axes)
        total = take(x, me)
        for k in range(1, n):
            total = total + lax.ppermute(take(x, (me + k) % n), axes, ring_pairs(n, k))
        outs.append(total)
    return outs


def direct_all_gather(jobs):
    outs = []
    for x, axes, n in jobs:
        me = lax.axis_index(axes)
        buf = put(jnp.zeros((n,) + x.shape, x.dtype), x, me)
        for k in range(1, n):
            buf = put(buf, lax.ppermute(x, axes, ring_pairs(n, k)), (me - k) % n)
        outs.append(buf)
    return outs


def on_device(region_factors, item_factors, slab_blocks, block_rows, counts):
    n_zh, n_x = lax.axis_size("zh"), lax.axis_size("x")
    n_zl, n_y, n_core = lax.axis_size("zl"), lax.axis_size("y"), lax.axis_size("core")
    block = slab_blocks.shape[-1]
    width = region_factors.shape[-1]
    jj = block // (n_zh * n_x)
    hw = width // 2
    row_blocks = region_factors.shape[0] // block
    region_blocks = region_factors.reshape(row_blocks, block, width)

    piece = item_factors[0]
    (got,) = direct_all_gather([(piece, "zh", n_zh)])
    (got,) = direct_all_gather([(got, "zl", n_zl)])
    part_a, part_b = direct_all_gather([(got[..., :hw], "x", n_x), (got[..., hw:], "y", n_y)])
    part_a, part_b = direct_all_gather([(part_a, "y", n_y), (part_b, "x", n_x)])
    part_a = part_a.transpose(0, 2, 3, 1, 4, 5)
    part_b = part_b.transpose(1, 2, 3, 0, 4, 5)
    panel_y = jnp.concatenate([part_a, part_b], axis=-1).reshape(n_y, n_zl, block, width)
    swap = ring_pairs(n_core, 1)
    panel_other = lax.ppermute(panel_y, "core", swap)

    me = lax.axis_index("core")
    tiles, rows_flat, live = slab_blocks[0], block_rows[0].reshape(-1), counts[0]
    partial_regions, other_part = local_grads(
        region_blocks, panel_other, tiles, rows_flat, live, (1 - me)[None], None, False
    )
    got = lax.ppermute(other_part, "core", swap)
    new_regions, own_part = local_grads(
        region_blocks, panel_y, tiles, rows_flat, live, me[None], partial_regions, True
    )

    own_part = own_part.reshape(n_y, n_zl, n_zh, n_x, jj, width)
    got = got.reshape(n_y, n_zl, n_zh, n_x, jj, width)
    part_a = own_part[..., :hw] + got[..., :hw]
    part_b = (own_part[..., hw:] + got[..., hw:]).transpose(3, 0, 1, 2, 4, 5)
    part_a, part_b = direct_reduce_scatter([(part_a, "y", n_y), (part_b, "x", n_x)])
    part_a = part_a.transpose(2, 0, 1, 3, 4)
    part_a, part_b = direct_reduce_scatter([(part_a, "x", n_x), (part_b, "y", n_y)])
    grad = jnp.concatenate([part_a, part_b], axis=-1)
    (grad,) = direct_reduce_scatter([(grad, "zl", n_zl)])
    (own_grad,) = direct_reduce_scatter([(grad, "zh", n_zh)])

    own_rows = piece.astype(jnp.float32)
    new_items = own_rows - item_rate * (own_grad + decay_rate * own_rows)
    return (new_regions.reshape(row_blocks * block, width), new_items[None])


def solution(mesh):
    rows, cols = mesh.devices.shape
    n_zh = 2
    n_core = 2
    n_x = rows // n_zh
    n_y = 4
    n_zl = cols // (n_y * n_core)
    fine = Mesh(mesh.devices.reshape(n_zh, n_x, n_zl, n_y, n_core), AXES)
    return jax.shard_map(
        on_device,
        mesh=fine,
        in_specs=(
            P(AXES, None),
            P(("zl", "y", "core"), ("zh", "x"), None),
            P(AXES, None, None, None, None),
            P(AXES, None, None),
            P(AXES, None),
        ),
        out_specs=(P(AXES, None), P(("zl", "y", "core"), ("zh", "x"), None)),
        check_vma=False,
    )
```
